512 devices in a mesh: section: 8 (over y, z_hi), space: 64 (over x, z_lo, core).
Axes of the slice: x: 4, y: 4, z: 16 (z_hi: 2, z_lo: 8; z = z_hi * 8 + z_lo), core: 2. Of those that a mesh axis runs over, the one named last changes fastest.
Arguments:
- nodes_in: bfloat16 [16, 8192, 256], P('section', 'space'), may hold values from -6 to 6
- edges_in: bfloat16 [16, 3, 8192, 256], P('section', None, 'space'), may hold values from -6 to 6
- codes: int32 [8192], P('space'), may hold values from 0 to 8
- type_table: float32 [9, 256], replicated, may hold values from -6 to 6
- order: int32 [16], replicated, may hold values from 0 to 15, as said below
- edge_w1: bfloat16 [8, 768, 256], P('section'), may hold values from -0.21875 to 0.21875
- edge_w2: bfloat16 [8, 256, 256], P('section'), may hold values from -0.375 to 0.375
- node_w1: bfloat16 [8, 512, 256], P('section'), may hold values from -0.25 to 0.25
- node_w2: bfloat16 [8, 256, 256], P('section'), may hold values from -0.375 to 0.375
- edge_v1: bfloat16 [8, 768, 256], P('section'), may hold values from -0.21875 to 0.21875
- edge_v2: bfloat16 [8, 256, 256], P('section'), may hold values from -0.375 to 0.375
- node_v1: bfloat16 [8, 512, 256], P('section'), may hold values from -0.25 to 0.25
- node_v2: bfloat16 [8, 256, 256], P('section'), may hold values from -0.375 to 0.375
Outputs:
- finished_nodes: bfloat16 [16, 8192, 256], P('section', 'space')
The draws below stay inside these ranges and needn't reach their ends.
Inputs may be any that keep to these rules, and one draw needn't show every extreme that they name: order names each micro-batch exactly once.
All inputs are finite; a program needn't handle non-finite values.
Results may differ from the reference program's by a relative error of at most 0.018.
Values may be sent and summed in bfloat16 or wider, within the bound.
No kernel may reach another device: no remote copies, remote signals or barrier semaphores. Data moves between devices by JAX's collectives and lax.ppermute only.
A program may use at most 64 MiB of HBM per device.

```python
import jax
import jax.numpy as jnp
from jax import lax

D = 256
NTYPES = 9
BX = 8
BY = 4
BZ = 4
NODES = 8192
M = 16
N_SECTION = 8
N_SPACE = 64


def draw_order(key, part):
    return jax.random.permutation(jax.random.fold_in(key, 17), M).astype(jnp.int32)


def with_ends(values, stream_key, least, largest):
    index_at = [jax.random.randint(jax.random.fold_in(stream_key, axis), (), 0, length) for axis, length in enumerate(values.shape)]
    longest = values.shape.index(max(values.shape))
    next_to = index_at[:longest] + [(index_at[longest] + 1) % values.shape[longest]] + index_at[longest + 1:]
    return values.at[tuple(index_at)].set(least).at[tuple(next_to)].set(largest)


def steps_of(key, shape, cuts, smallest, high):
    gain, own = 1.0, jax.random.fold_in(key, 6)
    for dim, shards_of in cuts:
        steps = jnp.exp(jax.random.uniform(jax.random.fold_in(own, dim), (shards_of,), jnp.float32, smallest / len(cuts), high / len(cuts)))
        gain = gain * jnp.repeat(steps, shape[dim] // shards_of).reshape([-1 if axis == dim else 1 for axis in range(len(shape))])
    return gain


def centred(key, shape, deviation, most, split=(), kind=jnp.bfloat16):
    loudness = steps_of(key, shape, split, -0.22, 0.18) if split else 1.0
    entries = jax.random.normal(key, shape, jnp.float32) * deviation * loudness
    return jnp.minimum(jnp.maximum(entries, -most), most).astype(kind)


def setup_inputs(seed: int = 0) -> dict:
    keys = jax.random.split(jax.random.key(seed), 14)
    nodes_in = centred(keys[0], (M, NODES, D), 1.0, 6.0, ((0, 8), (1, 64)))
    edges_in = centred(keys[1], (M, 3, NODES, D), 1.0, 6.0, ((0, 8), (2, 64)))
    codes = with_ends(jax.random.randint(keys[2], (NODES,), 0, NTYPES), jax.random.fold_in(keys[2], 1), 0, NTYPES - 1).astype(jnp.int32)
    type_table = centred(keys[3], (NTYPES, D), 1.0, 6.0, (), jnp.float32)
    order = draw_order(jax.random.fold_in(keys[13], 71), 0)
    edge_w1 = centred(keys[5], (N_SECTION, 3 * D, D), (3 * D) ** -0.5, 0.21875, ((0, 8),))
    edge_w2 = centred(keys[6], (N_SECTION, D, D), D ** -0.5, 0.375, ((0, 8),))
    node_w1 = centred(keys[7], (N_SECTION, 2 * D, D), (2 * D) ** -0.5, 0.25, ((0, 8),))
    node_w2 = centred(keys[8], (N_SECTION, D, D), D ** -0.5, 0.375, ((0, 8),))
    edge_v1 = centred(keys[9], (N_SECTION, 3 * D, D), (3 * D) ** -0.5, 0.21875, ((0, 8),))
    edge_v2 = centred(keys[10], (N_SECTION, D, D), D ** -0.5, 0.375, ((0, 8),))
    node_v1 = centred(keys[11], (N_SECTION, 2 * D, D), (2 * D) ** -0.5, 0.25, ((0, 8),))
    node_v2 = centred(keys[12], (N_SECTION, D, D), D ** -0.5, 0.375, ((0, 8),))
    return dict(nodes_in=nodes_in, edges_in=edges_in, codes=codes, type_table=type_table, order=order, edge_w1=edge_w1, edge_w2=edge_w2, node_w1=node_w1, node_w2=node_w2, edge_v1=edge_v1, edge_v2=edge_v2, node_v1=node_v1, node_v2=node_v2)


def layer_norm(values):
    centre = lax.optimization_barrier(jnp.mean(values, axis=-1, keepdims=True))
    spread = lax.optimization_barrier(jnp.mean((values - centre) * (values - centre), axis=-1, keepdims=True))
    return (values - centre) * lax.rsqrt(spread + 1e-05)

def predict(weight, velocity, scale_now):
    return (weight.astype(jnp.float32) + scale_now * velocity.astype(jnp.float32)).astype(jnp.bfloat16)

def to_grid(flat):
    count_z = N_SPACE // 16
    blocks = flat.reshape(4, 4, count_z, BX, BY, BZ, flat.shape[-1])
    blocks = jnp.transpose(blocks, (0, 3, 1, 4, 2, 5, 6))
    return blocks.reshape(4 * BX, 4 * BY, count_z * BZ, flat.shape[-1])

def from_grid(grid):
    count_z = N_SPACE // 16
    blocks = grid.reshape(4, BX, 4, BY, count_z, BZ, grid.shape[-1])
    blocks = jnp.transpose(blocks, (0, 2, 4, 1, 3, 5, 6))
    return blocks.reshape(NODES, grid.shape[-1])

def step_up(grid, axis_id):
    length = grid.shape[axis_id]
    return jnp.concatenate([lax.slice_in_dim(grid, 1, length, axis=axis_id), jnp.zeros_like(lax.slice_in_dim(grid, 0, 1, axis=axis_id))], axis=axis_id)

def step_down(grid, axis_id):
    length = grid.shape[axis_id]
    return jnp.concatenate([jnp.zeros_like(lax.slice_in_dim(grid, 0, 1, axis=axis_id)), lax.slice_in_dim(grid, 0, length - 1, axis=axis_id)], axis=axis_id)

def edge_update(edge_lat, node_src, node_dst, w_first, w_second):
    joined = jnp.concatenate([edge_lat, node_src, node_dst], axis=-1)
    hidden = jax.nn.relu(jnp.dot(joined, w_first, preferred_element_type=jnp.float32)).astype(jnp.bfloat16)
    result = jnp.dot(hidden, w_second, preferred_element_type=jnp.float32)
    return edge_lat.astype(jnp.float32) + layer_norm(result)

def grid_layer(node_lat, edges, type_embed, weights):
    ew_first, ew_second, nw_first, nw_second = weights
    total = jnp.zeros(node_lat.shape, jnp.float32)
    updated = []
    for axis_id in range(3):
        length = node_lat.shape[axis_id]
        exists = (lax.broadcasted_iota(jnp.int32, node_lat.shape[:3], axis_id) < length - 1)[..., None]
        fresh = edge_update(edges[axis_id], node_lat, step_up(node_lat, axis_id), ew_first, ew_second)
        fresh = jnp.where(exists, fresh, 0.0).astype(jnp.bfloat16)
        updated.append(fresh)
        total = total + fresh.astype(jnp.float32) + step_down(fresh, axis_id).astype(jnp.float32)
    joined = jnp.concatenate([node_lat, total.astype(jnp.bfloat16)], axis=-1)
    pre_act = jnp.dot(joined, nw_first, preferred_element_type=jnp.float32) + type_embed
    hidden = jax.nn.relu(pre_act).astype(jnp.bfloat16)
    result = jnp.dot(hidden, nw_second, preferred_element_type=jnp.float32)
    node_next = (node_lat.astype(jnp.float32) + layer_norm(result)).astype(jnp.bfloat16)
    return (node_next, jnp.stack(updated))

def reference(nodes_in, edges_in, codes, type_table, order, edge_w1, edge_w2, node_w1, node_w2, edge_v1, edge_v2, node_v1, node_v2):
    type_embed = to_grid(type_table[codes])
    section_ids = jnp.arange(N_SECTION, dtype=jnp.int32)

    def run_one(position):
        batch_id = order[position]
        node_lat = to_grid(nodes_in[batch_id])
        edges = jnp.stack([to_grid(edges_in[batch_id, axis_id]) for axis_id in range(3)])

        def layer_step(carry, layer_data):
            node_now, edge_now = carry
            layer_id, ew1, ew2, nw1, nw2, ev1, ev2, nv1, nv2 = layer_data
            scale_now = (position + 2 * N_SECTION - 2 - layer_id).astype(jnp.float32) / jnp.float32(M + 2 * N_SECTION)
            weights = (predict(ew1, ev1, scale_now), predict(ew2, ev2, scale_now), predict(nw1, nv1, scale_now), predict(nw2, nv2, scale_now))
            return (grid_layer(node_now, edge_now, type_embed, weights), None)
        (node_lat, edges), _ = lax.scan(layer_step, (node_lat, edges), (section_ids, edge_w1, edge_w2, node_w1, node_w2, edge_v1, edge_v2, node_v1, node_v2))
        return from_grid(node_lat)
    results = lax.map(run_one, jnp.arange(M, dtype=jnp.int32))
    return jnp.zeros_like(nodes_in).at[order].set(results)
```

```python
import jax
import jax.numpy as jnp
from jax import lax
from jax.sharding import PartitionSpec as P

BX = 8
BY = 4
BZ = 4


def from_behind(shard, axis, by):
    peers = lax.axis_size(axis)
    pairs = [(i, i + by) for i in range(peers) if 0 <= i + by < peers]
    return lax.ppermute(shard, axis, pairs)


def layer_norm(values):
    centre = jnp.mean(values, axis=-1, keepdims=True)
    spread = jnp.mean((values - centre) * (values - centre), axis=-1, keepdims=True)
    return (values - centre) * lax.rsqrt(spread + 1e-05)


def predict(weight, velocity, scales):
    return (
        weight.astype(jnp.float32)[None]
        + scales[:, None, None] * velocity.astype(jnp.float32)[None]
    ).astype(jnp.bfloat16)


def bmm(x, w):
    shape = x.shape
    flat = x.reshape(shape[0], -1, shape[-1])
    out = jnp.einsum("bnk,bkd->bnd", flat, w, preferred_element_type=jnp.float32)
    return out.reshape(shape[:-1] + (w.shape[-1],))


def edge_update(edge_lat, node_src, node_dst, w_first, w_second):
    joined = jnp.concatenate([edge_lat, node_src, node_dst], axis=-1)
    hidden = jax.nn.relu(bmm(joined, w_first)).astype(jnp.bfloat16)
    result = bmm(hidden, w_second)
    return edge_lat.astype(jnp.float32) + layer_norm(result)


def block_layer(node_lat, edges, weights, type_embed, coords, counts, strides):
    ew_first, ew_second, nw_first, nw_second = weights
    total = jnp.zeros(node_lat.shape, jnp.float32)
    updated = []
    for axis_id in range(3):
        ax = axis_id + 1
        length = node_lat.shape[ax]
        bottom = lax.slice_in_dim(node_lat, 0, 1, axis=ax)
        has_lower = coords[axis_id] > 0
        above = from_behind(bottom, "space", -strides[axis_id])
        node_next = jnp.concatenate(
            [lax.slice_in_dim(node_lat, 1, length, axis=ax), above], axis=ax
        )
        global_pos = coords[axis_id] * length + lax.broadcasted_iota(
            jnp.int32, node_lat.shape[:4], ax
        )
        exists = (global_pos < length * counts[axis_id] - 1)[..., None]
        fresh = edge_update(edges[axis_id], node_lat, node_next, ew_first, ew_second)
        fresh = jnp.where(exists, fresh, 0.0).astype(jnp.bfloat16)
        below = from_behind(
            lax.slice_in_dim(fresh, length - 1, length, axis=ax), "space", strides[axis_id]
        )
        below = jnp.where(has_lower, below, jnp.zeros_like(below))
        before = jnp.concatenate(
            [below, lax.slice_in_dim(fresh, 0, length - 1, axis=ax)], axis=ax
        )
        updated.append(fresh)
        total = total + fresh.astype(jnp.float32) + before.astype(jnp.float32)
    joined = jnp.concatenate([node_lat, total.astype(jnp.bfloat16)], axis=-1)
    pre_act = bmm(joined, nw_first) + type_embed
    hidden = jax.nn.relu(pre_act).astype(jnp.bfloat16)
    result = bmm(hidden, nw_second)
    node_next_lat = (node_lat.astype(jnp.float32) + layer_norm(result)).astype(jnp.bfloat16)
    return node_next_lat, updated


def local(
    nodes_in,
    edges_in,
    codes,
    type_table,
    order,
    edge_w1,
    edge_w2,
    node_w1,
    node_w2,
    edge_v1,
    edge_v2,
    node_v1,
    node_v2,
):
    section_count = lax.axis_size("section")
    section_id = lax.axis_index("section")
    count_z = lax.axis_size("space") // 16
    space_id = lax.axis_index("space")
    coords = (space_id // (4 * count_z), space_id // count_z % 4, space_id % count_z)
    counts = (4, 4, count_z)
    strides = (4 * count_z, count_z, 1)
    width = nodes_in.shape[-1]
    local_count = nodes_in.shape[0]
    batches = local_count * section_count
    type_ids = lax.broadcasted_iota(jnp.int32, (codes.shape[0], type_table.shape[0]), 1)
    one_hot = (codes[:, None] == type_ids).astype(jnp.float32)
    type_embed = jnp.sum(one_hot[:, :, None] * type_table[None, :, :], axis=1).reshape(
        BX, BY, BZ, width
    )
    divisor = jnp.float32(batches + 2 * section_count)

    mine = section_id * local_count + jnp.arange(local_count, dtype=jnp.int32)
    slots = jnp.arange(batches, dtype=jnp.int32)
    position = jnp.sum(
        jnp.where(order[None, :] == mine[:, None], slots[None, :], 0), axis=1
    )

    gathered = [
        lax.all_gather(w[0], "section", axis=0, tiled=False)
        for w in (edge_w1, edge_w2, node_w1, node_w2, edge_v1, edge_v2, node_v1, node_v2)
    ]

    node_lat = nodes_in.reshape(local_count, BX, BY, BZ, width)
    edges = tuple(
        edges_in[:, a].reshape(local_count, BX, BY, BZ, width) for a in range(3)
    )

    def layer_step(layer_id, carry):
        node_now, edge_now = carry
        scales = (position + 2 * section_count - 2 - layer_id).astype(jnp.float32) / divisor
        picked = [lax.dynamic_index_in_dim(g, layer_id, 0, False) for g in gathered]
        weights = tuple(predict(picked[i], picked[i + 4], scales) for i in range(4))
        node_next, updated = block_layer(
            node_now, edge_now, weights, type_embed, coords, counts, strides
        )
        return (node_next, tuple(updated))

    node_lat, _ = lax.fori_loop(0, section_count, layer_step, (node_lat, edges))
    return node_lat.reshape(nodes_in.shape)


def solution(mesh):
    return jax.shard_map(
        local,
        mesh=mesh,
        in_specs=(
            P("section", "space", None),
            P("section", None, "space", None),
            P("space"),
            P(),
            P(),
            P("section", None, None),
            P("section", None, None),
            P("section", None, None),
            P("section", None, None),
            P("section", None, None),
            P("section", None, None),
            P("section", None, None),
            P("section", None, None),
        ),
        out_specs=P("section", "space", None),
        check_vma=False,
    )
```

```python
import jax
import jax.numpy as jnp
from jax import lax
from jax.sharding import PartitionSpec as P

BX = 8
BY = 4
BZ = 4


def from_behind(shard, axis, by):
    peers = lax.axis_size(axis)
    pairs = [(i, i + by) for i in range(peers) if 0 <= i + by < peers]
    return lax.ppermute(shard, axis, pairs)


def layer_norm(values):
    centre = jnp.mean(values, axis=-1, keepdims=True)
    spread = jnp.mean((values - centre) * (values - centre), axis=-1, keepdims=True)
    return (values - centre) * lax.rsqrt(spread + 1e-05)


def predict(weight, velocity, scales):
    return (
        weight.astype(jnp.float32)[None]
        + scales[:, None, None] * velocity.astype(jnp.float32)[None]
    ).astype(jnp.bfloat16)


def bmm(x, w):
    shape = x.shape
    flat = x.reshape(shape[0], -1, shape[-1])
    out = jnp.einsum("bnk,bkd->bnd", flat, w, preferred_element_type=jnp.float32)
    return out.reshape(shape[:-1] + (w.shape[-1],))


def edge_update(edge_lat, node_src, node_dst, w_first, w_second):
    joined = jnp.concatenate([edge_lat, node_src, node_dst], axis=-1)
    hidden = jax.nn.relu(bmm(joined, w_first)).astype(jnp.bfloat16)
    result = bmm(hidden, w_second)
    return edge_lat.astype(jnp.float32) + layer_norm(result)


def block_layer(node_lat, edges, weights, type_embed, coords, counts, strides):
    ew_first, ew_second, nw_first, nw_second = weights
    total = jnp.zeros(node_lat.shape, jnp.float32)
    updated = []
    for axis_id in range(3):
        ax = axis_id + 1
        length = node_lat.shape[ax]
        bottom = lax.slice_in_dim(node_lat, 0, 1, axis=ax)
        has_lower = coords[axis_id] > 0
        above = from_behind(bottom, "space", -strides[axis_id])
        node_next = jnp.concatenate(
            [lax.slice_in_dim(node_lat, 1, length, axis=ax), above], axis=ax
        )
        global_pos = coords[axis_id] * length + lax.broadcasted_iota(
            jnp.int32, node_lat.shape[:4], ax
        )
        exists = (global_pos < length * counts[axis_id] - 1)[..., None]
        fresh = edge_update(edges[axis_id], node_lat, node_next, ew_first, ew_second)
        fresh = jnp.where(exists, fresh, 0.0).astype(jnp.bfloat16)
        below = from_behind(
            lax.slice_in_dim(fresh, length - 1, length, axis=ax), "space", strides[axis_id]
        )
        below = jnp.where(has_lower, below, jnp.zeros_like(below))
        before = jnp.concatenate(
            [below, lax.slice_in_dim(fresh, 0, length - 1, axis=ax)], axis=ax
        )
        updated.append(fresh)
        total = total + fresh.astype(jnp.float32) + before.astype(jnp.float32)
    joined = jnp.concatenate([node_lat, total.astype(jnp.bfloat16)], axis=-1)
    pre_act = bmm(joined, nw_first) + type_embed
    hidden = jax.nn.relu(pre_act).astype(jnp.bfloat16)
    result = bmm(hidden, nw_second)
    node_next_lat = (node_lat.astype(jnp.float32) + layer_norm(result)).astype(jnp.bfloat16)
    return node_next_lat, updated


def local(
    nodes_in,
    edges_in,
    codes,
    type_table,
    order,
    edge_w1,
    edge_w2,
    node_w1,
    node_w2,
    edge_v1,
    edge_v2,
    node_v1,
    node_v2,
):
    section_count = lax.axis_size("section")
    section_id = lax.axis_index("section")
    count_z = lax.axis_size("space") // 16
    space_id = lax.axis_index("space")
    coords = (space_id // (4 * count_z), space_id // count_z % 4, space_id % count_z)
    counts = (4, 4, count_z)
    strides = (4 * count_z, count_z, 1)
    width = nodes_in.shape[-1]
    local_count = nodes_in.shape[0]
    batches = local_count * section_count
    type_ids = lax.broadcasted_iota(jnp.int32, (codes.shape[0], type_table.shape[0]), 1)
    one_hot = (codes[:, None] == type_ids).astype(jnp.float32)
    type_embed = jnp.sum(one_hot[:, :, None] * type_table[None, :, :], axis=1).reshape(
        BX, BY, BZ, width
    )
    divisor = jnp.float32(batches + 2 * section_count)

    mine = section_id * local_count + jnp.arange(local_count, dtype=jnp.int32)
    slots = jnp.arange(batches, dtype=jnp.int32)
    position = jnp.sum(
        jnp.where(order[None, :] == mine[:, None], slots[None, :], 0), axis=1
    )

    core = space_id % 2
    sizes = [w.shape[1] for w in (edge_w1, edge_w2, node_w1, node_w2)]
    halves = (
        jnp.concatenate([edge_w1[0], edge_w2[0], node_w1[0], node_w2[0]], axis=0),
        jnp.concatenate([edge_v1[0], edge_v2[0], node_v1[0], node_v2[0]], axis=0),
    )
    own_half = jnp.where(core == 0, halves[0], halves[1])
    own_all = lax.all_gather(own_half, "section", axis=0, tiled=False)
    space_count = lax.axis_size("space")
    swap = [(i, i ^ 1) for i in range(space_count)]
    other_all = lax.ppermute(own_all, "space", swap)
    starts = [sum(sizes[:i]) for i in range(4)]

    node_lat = nodes_in.reshape(local_count, BX, BY, BZ, width)
    edges = tuple(
        edges_in[:, a].reshape(local_count, BX, BY, BZ, width) for a in range(3)
    )

    def layer_step(layer_id, carry):
        node_now, edge_now = carry
        scales = (position + 2 * section_count - 2 - layer_id).astype(jnp.float32) / divisor
        mine_now = lax.dynamic_index_in_dim(own_all, layer_id, 0, False)
        other_now = lax.dynamic_index_in_dim(other_all, layer_id, 0, False)
        w_now = jnp.where(core == 0, mine_now, other_now)
        v_now = jnp.where(core == 0, other_now, mine_now)
        weights = tuple(
            predict(
                lax.slice_in_dim(w_now, starts[i], starts[i] + sizes[i], axis=0),
                lax.slice_in_dim(v_now, starts[i], starts[i] + sizes[i], axis=0),
                scales,
            )
            for i in range(4)
        )
        node_next, updated = block_layer(
            node_now, edge_now, weights, type_embed, coords, counts, strides
        )
        return (node_next, tuple(updated))

    node_lat, _ = lax.fori_loop(0, section_count, layer_step, (node_lat, edges))
    return node_lat.reshape(nodes_in.shape)


def solution(mesh):
    return jax.shard_map(
        local,
        mesh=mesh,
        in_specs=(
            P("section", "space", None),
            P("section", None, "space", None),
            P("space"),
            P(),
            P(),
            P("section", None, None),
            P("section", None, None),
            P("section", None, None),
            P("section", None, None),
            P("section", None, None),
            P("section", None, None),
            P("section", None, None),
            P("section", None, None),
        ),
        out_specs=P("section", "space", None),
        check_vma=False,
    )
```

```python
import jax
import jax.numpy as jnp
from jax import lax
from jax.sharding import PartitionSpec as P

BX = 8
BY = 4
BZ = 4


def from_behind(shard, axis, by):
    peers = lax.axis_size(axis)
    pairs = [(i, i + by) for i in range(peers) if 0 <= i + by < peers]
    return lax.ppermute(shard, axis, pairs)


def layer_norm(values):
    centre = jnp.mean(values, axis=-1, keepdims=True)
    spread = jnp.mean((values - centre) * (values - centre), axis=-1, keepdims=True)
    return (values - centre) * lax.rsqrt(spread + 1e-05)


def predict(weight, velocity, scales):
    return (
        weight.astype(jnp.float32)[None]
        + scales[:, None, None] * velocity.astype(jnp.float32)[None]
    ).astype(jnp.bfloat16)


def bmm(x, w):
    shape = x.shape
    flat = x.reshape(shape[0], -1, shape[-1])
    out = jnp.einsum("bnk,bkd->bnd", flat, w, preferred_element_type=jnp.float32)
    return out.reshape(shape[:-1] + (w.shape[-1],))


def edge_update(edge_lat, node_src, node_dst, w_first, w_second):
    joined = jnp.concatenate([edge_lat, node_src, node_dst], axis=-1)
    hidden = jax.nn.relu(bmm(joined, w_first)).astype(jnp.bfloat16)
    result = bmm(hidden, w_second)
    return edge_lat.astype(jnp.float32) + layer_norm(result)


def block_layer(node_lat, edges, ghosts, weights, type_embed, coords, counts, strides):
    ew_first, ew_second, nw_first, nw_second = weights
    batch, width = node_lat.shape[0], node_lat.shape[-1]
    pieces = []
    for axis_id in range(3):
        ax = axis_id + 1
        length = node_lat.shape[ax]
        bottom = lax.slice_in_dim(node_lat, 0, 1, axis=ax)
        top = lax.slice_in_dim(node_lat, length - 1, length, axis=ax)
        above = from_behind(bottom, "space", -strides[axis_id])
        below = from_behind(top, "space", strides[axis_id])
        node_next = jnp.concatenate(
            [lax.slice_in_dim(node_lat, 1, length, axis=ax), above], axis=ax
        )
        pieces.append((edges[axis_id], node_lat, node_next))
        pieces.append((ghosts[axis_id], below, bottom))
    rows = [p[0].size // (batch * width) for p in pieces]
    joined = jnp.concatenate(
        [
            jnp.concatenate([e, s, d], axis=-1).reshape(batch, r, 3 * width)
            for (e, s, d), r in zip(pieces, rows)
        ],
        axis=1,
    )
    edge_all = jnp.concatenate(
        [p[0].reshape(batch, r, width) for p, r in zip(pieces, rows)], axis=1
    )
    hidden = jax.nn.relu(bmm(joined, ew_first)).astype(jnp.bfloat16)
    result = bmm(hidden, ew_second)
    fresh_all = edge_all.astype(jnp.float32) + layer_norm(result)

    total = jnp.zeros(node_lat.shape, jnp.float32)
    updated = []
    new_ghosts = []
    offset = 0
    for axis_id in range(3):
        ax = axis_id + 1
        length = node_lat.shape[ax]
        own_rows, ghost_rows = rows[2 * axis_id], rows[2 * axis_id + 1]
        fresh = lax.slice_in_dim(fresh_all, offset, offset + own_rows, axis=1).reshape(
            node_lat.shape
        )
        offset += own_rows
        ghost = lax.slice_in_dim(fresh_all, offset, offset + ghost_rows, axis=1).reshape(
            ghosts[axis_id].shape
        )
        offset += ghost_rows
        global_pos = coords[axis_id] * length + lax.broadcasted_iota(
            jnp.int32, node_lat.shape[:4], ax
        )
        exists = (global_pos < length * counts[axis_id] - 1)[..., None]
        fresh = jnp.where(exists, fresh, 0.0).astype(jnp.bfloat16)
        has_lower = coords[axis_id] > 0
        ghost = jnp.where(has_lower, ghost, 0.0).astype(jnp.bfloat16)
        before = jnp.concatenate(
            [ghost, lax.slice_in_dim(fresh, 0, length - 1, axis=ax)], axis=ax
        )
        updated.append(fresh)
        new_ghosts.append(ghost)
        total = total + fresh.astype(jnp.float32) + before.astype(jnp.float32)
    joined = jnp.concatenate([node_lat, total.astype(jnp.bfloat16)], axis=-1)
    pre_act = bmm(joined, nw_first) + type_embed
    hidden = jax.nn.relu(pre_act).astype(jnp.bfloat16)
    result = bmm(hidden, nw_second)
    node_next_lat = (node_lat.astype(jnp.float32) + layer_norm(result)).astype(jnp.bfloat16)
    return node_next_lat, updated, new_ghosts


def local(
    nodes_in,
    edges_in,
    codes,
    type_table,
    order,
    edge_w1,
    edge_w2,
    node_w1,
    node_w2,
    edge_v1,
    edge_v2,
    node_v1,
    node_v2,
):
    section_count = lax.axis_size("section")
    section_id = lax.axis_index("section")
    count_z = lax.axis_size("space") // 16
    space_id = lax.axis_index("space")
    coords = (space_id // (4 * count_z), space_id // count_z % 4, space_id % count_z)
    counts = (4, 4, count_z)
    strides = (4 * count_z, count_z, 1)
    width = nodes_in.shape[-1]
    local_count = nodes_in.shape[0]
    batches = local_count * section_count
    type_ids = lax.broadcasted_iota(jnp.int32, (codes.shape[0], type_table.shape[0]), 1)
    one_hot = (codes[:, None] == type_ids).astype(jnp.float32)
    type_embed = jnp.sum(one_hot[:, :, None] * type_table[None, :, :], axis=1).reshape(
        BX, BY, BZ, width
    )
    divisor = jnp.float32(batches + 2 * section_count)

    mine = section_id * local_count + jnp.arange(local_count, dtype=jnp.int32)
    slots = jnp.arange(batches, dtype=jnp.int32)
    position = jnp.sum(
        jnp.where(order[None, :] == mine[:, None], slots[None, :], 0), axis=1
    )

    core = space_id % 2
    sizes = [w.shape[1] for w in (edge_w1, edge_w2, node_w1, node_w2)]
    halves = (
        jnp.concatenate([edge_w1[0], edge_w2[0], node_w1[0], node_w2[0]], axis=0),
        jnp.concatenate([edge_v1[0], edge_v2[0], node_v1[0], node_v2[0]], axis=0),
    )
    own_half = jnp.where(core == 0, halves[0], halves[1])
    own_all = lax.all_gather(own_half, "section", axis=0, tiled=False)
    space_count = lax.axis_size("space")
    swap = [(i, i ^ 1) for i in range(space_count)]
    other_all = lax.ppermute(own_all, "space", swap)
    starts = [sum(sizes[:i]) for i in range(4)]

    node_lat = nodes_in.reshape(local_count, BX, BY, BZ, width)
    edges = tuple(
        edges_in[:, a].reshape(local_count, BX, BY, BZ, width) for a in range(3)
    )

    ghosts = tuple(
        from_behind(
            lax.slice_in_dim(edges[a], edges[a].shape[a + 1] - 1, edges[a].shape[a + 1], axis=a + 1),
            "space",
            strides[a],
        )
        for a in range(3)
    )

    def layer_step(layer_id, carry):
        node_now, edge_now, ghost_now = carry
        scales = (position + 2 * section_count - 2 - layer_id).astype(jnp.float32) / divisor
        mine_now = lax.dynamic_index_in_dim(own_all, layer_id, 0, False)
        other_now = lax.dynamic_index_in_dim(other_all, layer_id, 0, False)
        w_now = jnp.where(core == 0, mine_now, other_now)
        v_now = jnp.where(core == 0, other_now, mine_now)
        weights = tuple(
            predict(
                lax.slice_in_dim(w_now, starts[i], starts[i] + sizes[i], axis=0),
                lax.slice_in_dim(v_now, starts[i], starts[i] + sizes[i], axis=0),
                scales,
            )
            for i in range(4)
        )
        node_next, updated, new_ghosts = block_layer(
            node_now, edge_now, ghost_now, weights, type_embed, coords, counts, strides
        )
        return (node_next, tuple(updated), tuple(new_ghosts))

    node_lat, _, _ = lax.fori_loop(0, section_count, layer_step, (node_lat, edges, ghosts))
    return node_lat.reshape(nodes_in.shape)


def solution(mesh):
    return jax.shard_map(
        local,
        mesh=mesh,
        in_specs=(
            P("section", "space", None),
            P("section", None, "space", None),
            P("space"),
            P(),
            P(),
            P("section", None, None),
            P("section", None, None),
            P("section", None, None),
            P("section", None, None),
            P("section", None, None),
            P("section", None, None),
            P("section", None, None),
            P("section", None, None),
        ),
        out_specs=P("section", "space", None),
        check_vma=False,
    )
```

```python
import jax
import jax.numpy as jnp
from jax import lax
from jax.sharding import PartitionSpec as P
from jax.experimental import pallas as pl
import numpy as np

BX = 8
BY = 4
BZ = 4


def from_behind(shard, axis, by):
    peers = lax.axis_size(axis)
    pairs = [(i, i + by) for i in range(peers) if 0 <= i + by < peers]
    return lax.ppermute(shard, axis, pairs)


def layer_norm(values):
    centre = jnp.mean(values, axis=-1, keepdims=True)
    spread = jnp.mean((values - centre) * (values - centre), axis=-1, keepdims=True)
    return (values - centre) * lax.rsqrt(spread + 1e-05)


def predict(weight, velocity, scales):
    return (
        weight.astype(jnp.float32)[None]
        + scales[:, None, None] * velocity.astype(jnp.float32)[None]
    ).astype(jnp.bfloat16)


def plane_mats(shape):
    rows = int(np.prod(shape))
    coords = np.stack(np.unravel_index(np.arange(rows), shape), axis=1)
    strides = [int(np.prod(shape[a + 1:])) for a in range(3)]
    out = []
    for a in range(3):
        length = shape[a]
        plane = np.cumsum(coords[:, a] == 0) - 1
        index = np.zeros(rows, np.int64)
        for edge in range(length):
            picked = np.nonzero(coords[:, a] == edge)[0]
            index[picked] = np.arange(picked.size)
        count = rows // length
        bot = np.zeros((count, rows), np.float32)
        top = np.zeros((count, rows), np.float32)
        up = np.zeros((rows, rows), np.float32)
        t_up = np.zeros((rows, count), np.float32)
        down = np.zeros((rows, rows), np.float32)
        t_down = np.zeros((rows, count), np.float32)
        for r in range(rows):
            c = coords[r, a]
            if c == 0:
                bot[index[r], r] = 1
                t_down[r, index[r]] = 1
            else:
                down[r, r - strides[a]] = 1
            if c == length - 1:
                top[index[r], r] = 1
                t_up[r, index[r]] = 1
            else:
                up[r, r + strides[a]] = 1
        out.append(
            tuple(jnp.asarray(m, jnp.bfloat16) for m in (bot, top, up, t_up, down, t_down))
        )
    return out


def dot(a, b):
    return jnp.dot(a, b, preferred_element_type=jnp.float32)


def layer_kernel(*refs):
    (h_ref, e_ref, g0, g1, g2, a0, a1, a2, b0, b1, b2, temb_ref, w1_ref, w2_ref, n1_ref, n2_ref,
     omask_ref, m0, m1, m2) = refs[:20]
    mats = refs[20:38]
    outs = refs[38:]
    h_out, e_out = outs[0], outs[1]
    g_out = outs[2:5]
    bot_out = outs[5:8]
    top_out = outs[8:11]
    ghosts = (g0, g1, g2)
    aboves = (a0, a1, a2)
    belows = (b0, b1, b2)
    gmasks = (m0, m1, m2)
    width = h_ref.shape[-1]
    for b in range(h_ref.shape[0]):
        h = h_ref[b]
        w1 = w1_ref[b]
        w1e, w1s, w1d = w1[:width], w1[width:2 * width], w1[2 * width:]
        w2 = w2_ref[b]
        h_src = dot(h, w1s)
        total = jnp.zeros(h.shape, jnp.float32)
        for d in range(3):
            bot, top, up, t_up, down, t_down = (m[...] for m in mats[6 * d:6 * d + 6])
            e = e_ref[d, b]
            nxt = (dot(up, h) + dot(t_up, aboves[d][b])).astype(jnp.bfloat16)
            pre = dot(e, w1e) + h_src + dot(nxt, w1d)
            hid = jnp.maximum(pre, 0.0).astype(jnp.bfloat16)
            fresh = e.astype(jnp.float32) + layer_norm(dot(hid, w2))
            fresh = jnp.where(omask_ref[d] > 0.5, fresh, 0.0).astype(jnp.bfloat16)
            g = ghosts[d][b]
            bottom = dot(bot, h).astype(jnp.bfloat16)
            pre_g = dot(g, w1e) + dot(belows[d][b], w1s) + dot(bottom, w1d)
            hid_g = jnp.maximum(pre_g, 0.0).astype(jnp.bfloat16)
            ghost = g.astype(jnp.float32) + layer_norm(dot(hid_g, w2))
            ghost = jnp.where(gmasks[d][...] > 0.5, ghost, 0.0).astype(jnp.bfloat16)
            before = dot(down, fresh) + dot(t_down, ghost)
            total = total + fresh.astype(jnp.float32) + before
            e_out[d, b] = fresh
            g_out[d][b] = ghost
        n1 = n1_ref[b]
        pre = dot(h, n1[:width]) + dot(total.astype(jnp.bfloat16), n1[width:]) + temb_ref[...]
        hid = jnp.maximum(pre, 0.0).astype(jnp.bfloat16)
        h_new = (h.astype(jnp.float32) + layer_norm(dot(hid, n2_ref[b]))).astype(jnp.bfloat16)
        h_out[b] = h_new
        for d in range(3):
            bot, top = mats[6 * d][...], mats[6 * d + 1][...]
            bot_out[d][b] = dot(bot, h_new).astype(jnp.bfloat16)
            top_out[d][b] = dot(top, h_new).astype(jnp.bfloat16)


def run_layer(h, e, ghosts, aboves, belows, temb, weights, omask, gmasks, mats):
    batch, rows, width = h.shape
    counts = [g.shape[1] for g in ghosts]
    out_shape = (
        [jax.ShapeDtypeStruct(h.shape, h.dtype), jax.ShapeDtypeStruct(e.shape, e.dtype)]
        + [jax.ShapeDtypeStruct(g.shape, g.dtype) for g in ghosts]
        + [jax.ShapeDtypeStruct((batch, c, width), h.dtype) for c in counts] * 2
    )
    flat_mats = [m for group in mats for m in group]
    res = pl.pallas_call(layer_kernel, out_shape=out_shape)(
        h, e, *ghosts, *aboves, *belows, temb, *weights, omask, *gmasks, *flat_mats
    )
    return res[0], res[1], tuple(res[2:5]), tuple(res[5:8]), tuple(res[8:11])


def local(
    nodes_in,
    edges_in,
    codes,
    type_table,
    order,
    edge_w1,
    edge_w2,
    node_w1,
    node_w2,
    edge_v1,
    edge_v2,
    node_v1,
    node_v2,
):
    section_count = lax.axis_size("section")
    section_id = lax.axis_index("section")
    count_z = lax.axis_size("space") // 16
    space_id = lax.axis_index("space")
    coords = (space_id // (4 * count_z), space_id // count_z % 4, space_id % count_z)
    counts = (4, 4, count_z)
    strides = (4 * count_z, count_z, 1)
    width = nodes_in.shape[-1]
    local_count = nodes_in.shape[0]
    rows = nodes_in.shape[1]
    batches = local_count * section_count
    type_ids = lax.broadcasted_iota(jnp.int32, (codes.shape[0], type_table.shape[0]), 1)
    one_hot = (codes[:, None] == type_ids).astype(jnp.float32)
    type_embed = jnp.sum(one_hot[:, :, None] * type_table[None, :, :], axis=1)
    divisor = jnp.float32(batches + 2 * section_count)

    mine = section_id * local_count + jnp.arange(local_count, dtype=jnp.int32)
    slots = jnp.arange(batches, dtype=jnp.int32)
    position = jnp.sum(
        jnp.where(order[None, :] == mine[:, None], slots[None, :], 0), axis=1
    )

    core = space_id % 2
    sizes = [w.shape[1] for w in (edge_w1, edge_w2, node_w1, node_w2)]
    halves = (
        jnp.concatenate([edge_w1[0], edge_w2[0], node_w1[0], node_w2[0]], axis=0),
        jnp.concatenate([edge_v1[0], edge_v2[0], node_v1[0], node_v2[0]], axis=0),
    )
    own_half = jnp.where(core == 0, halves[0], halves[1])
    own_all = lax.all_gather(own_half, "section", axis=0, tiled=False)
    space_count = lax.axis_size("space")
    swap = [(i, i ^ 1) for i in range(space_count)]
    other_all = lax.ppermute(own_all, "space", swap)
    starts = [sum(sizes[:i]) for i in range(4)]

    shape = (BX, BY, BZ)
    mats = plane_mats(shape)
    grid_pos = np.stack(np.unravel_index(np.arange(rows), shape), axis=1)
    omask = jnp.stack(
        [
            jnp.broadcast_to(
                (coords[a] * shape[a] + grid_pos[:, a] < shape[a] * counts[a] - 1)[:, None],
                (rows, width),
            ).astype(jnp.float32)
            for a in range(3)
        ]
    )
    gmasks = tuple(
        jnp.broadcast_to(coords[a] > 0, (rows // shape[a], width)).astype(jnp.float32)
        for a in range(3)
    )

    h0 = nodes_in
    e0 = jnp.transpose(edges_in, (1, 0, 2, 3))
    bot0 = tuple(jnp.einsum("pr,brw->bpw", mats[a][0], h0).astype(jnp.bfloat16) for a in range(3))
    top0 = tuple(jnp.einsum("pr,brw->bpw", mats[a][1], h0).astype(jnp.bfloat16) for a in range(3))
    ghosts0 = tuple(
        from_behind(
            jnp.einsum("pr,brw->bpw", mats[a][1], e0[a]).astype(jnp.bfloat16),
            "space",
            strides[a],
        )
        for a in range(3)
    )

    def layer_step(layer_id, carry):
        h, e, ghosts, bots, tops = carry
        scales = (position + 2 * section_count - 2 - layer_id).astype(jnp.float32) / divisor
        mine_now = lax.dynamic_index_in_dim(own_all, layer_id, 0, False)
        other_now = lax.dynamic_index_in_dim(other_all, layer_id, 0, False)
        w_now = jnp.where(core == 0, mine_now, other_now)
        v_now = jnp.where(core == 0, other_now, mine_now)
        weights = tuple(
            predict(
                lax.slice_in_dim(w_now, starts[i], starts[i] + sizes[i], axis=0),
                lax.slice_in_dim(v_now, starts[i], starts[i] + sizes[i], axis=0),
                scales,
            )
            for i in range(4)
        )
        aboves = tuple(from_behind(bots[a], "space", -strides[a]) for a in range(3))
        belows = tuple(from_behind(tops[a], "space", strides[a]) for a in range(3))
        return run_layer(h, e, ghosts, aboves, belows, type_embed, weights, omask, gmasks, mats)

    h, _, _, _, _ = lax.fori_loop(
        0, section_count, layer_step, (h0, e0, ghosts0, bot0, top0)
    )
    return h


def solution(mesh):
    return jax.shard_map(
        local,
        mesh=mesh,
        in_specs=(
            P("section", "space", None),
            P("section", None, "space", None),
            P("space"),
            P(),
            P(),
            P("section", None, None),
            P("section", None, None),
            P("section", None, None),
            P("section", None, None),
            P("section", None, None),
            P("section", None, None),
            P("section", None, None),
            P("section", None, None),
        ),
        out_specs=P("section", "space", None),
        check_vma=False,
    )
```

```python
import jax
import jax.numpy as jnp
from jax import lax
from jax.sharding import PartitionSpec as P
from jax.experimental import pallas as pl
from jax.experimental.pallas import tpu as pltpu
import numpy as np

BX = 8
BY = 4
BZ = 4


def from_behind(shard, axis, by):
    peers = lax.axis_size(axis)
    pairs = [(i, i + by) for i in range(peers) if 0 <= i + by < peers]
    return lax.ppermute(shard, axis, pairs)


def layer_norm(values):
    centre = jnp.mean(values, axis=-1, keepdims=True)
    spread = jnp.mean((values - centre) * (values - centre), axis=-1, keepdims=True)
    return (values - centre) * lax.rsqrt(spread + 1e-05)


def predict(weight, velocity, scales):
    return (
        weight.astype(jnp.float32)[None]
        + scales[:, None, None] * velocity.astype(jnp.float32)[None]
    ).astype(jnp.bfloat16)


def plane_mats(shape):
    rows = int(np.prod(shape))
    coords = np.stack(np.unravel_index(np.arange(rows), shape), axis=1)
    strides = [int(np.prod(shape[a + 1:])) for a in range(3)]
    out = []
    for a in range(3):
        length = shape[a]
        plane = np.cumsum(coords[:, a] == 0) - 1
        index = np.zeros(rows, np.int64)
        for edge in range(length):
            picked = np.nonzero(coords[:, a] == edge)[0]
            index[picked] = np.arange(picked.size)
        count = rows // length
        bot = np.zeros((count, rows), np.float32)
        top = np.zeros((count, rows), np.float32)
        up = np.zeros((rows, rows), np.float32)
        t_up = np.zeros((rows, count), np.float32)
        down = np.zeros((rows, rows), np.float32)
        t_down = np.zeros((rows, count), np.float32)
        for r in range(rows):
            c = coords[r, a]
            if c == 0:
                bot[index[r], r] = 1
                t_down[r, index[r]] = 1
            else:
                down[r, r - strides[a]] = 1
            if c == length - 1:
                top[index[r], r] = 1
                t_up[r, index[r]] = 1
            else:
                up[r, r + strides[a]] = 1
        out.append(
            tuple(jnp.asarray(m, jnp.bfloat16) for m in (bot, top, up, t_up, down, t_down))
        )
    return out


def dot(a, b):
    return jnp.dot(a, b, preferred_element_type=jnp.float32)


def layer_kernel(*refs):
    idx = refs[0]
    (h_ref, e_ref, g0, g1, g2, a0, a1, a2, b0, b1, b2, temb_ref, mine_ref, other_ref, scale_ref,
     omask_ref) = refs[1:17]
    mats = refs[17:35]
    outs = refs[35:]
    h_out, e_out = outs[0], outs[1]
    g_out = outs[2:5]
    bot_out = outs[5:8]
    top_out = outs[8:11]
    ghosts = (g0, g1, g2)
    aboves = (a0, a1, a2)
    belows = (b0, b1, b2)
    width = h_ref.shape[-1]
    sizes = (3 * width, width, 2 * width, width)
    starts = [sum(sizes[:i]) for i in range(4)]
    core_zero = idx[1] == 0
    mine = mine_ref[0]
    other = other_ref[0]
    w_all = jnp.where(core_zero, mine, other).astype(jnp.float32)
    v_all = jnp.where(core_zero, other, mine).astype(jnp.float32)
    for b in range(h_ref.shape[0]):
        scale = scale_ref[b:b + 1, :]
        pred = (w_all + scale * v_all).astype(jnp.bfloat16)
        w1, w2, n1, n2 = (pred[starts[i]:starts[i] + sizes[i]] for i in range(4))
        h = h_ref[b]
        w1e, w1s, w1d = w1[:width], w1[width:2 * width], w1[2 * width:]
        h_src = dot(h, w1s)
        total = jnp.zeros(h.shape, jnp.float32)
        for d in range(3):
            bot, top, up, t_up, down, t_down = (m[...] for m in mats[6 * d:6 * d + 6])
            e = e_ref[d, b]
            nxt = (dot(up, h) + dot(t_up, aboves[d][b])).astype(jnp.bfloat16)
            pre = dot(e, w1e) + h_src + dot(nxt, w1d)
            hid = jnp.maximum(pre, 0.0).astype(jnp.bfloat16)
            fresh = e.astype(jnp.float32) + layer_norm(dot(hid, w2))
            fresh = jnp.where(omask_ref[d] > 0.5, fresh, 0.0).astype(jnp.bfloat16)
            g = ghosts[d][b]
            bottom = dot(bot, h).astype(jnp.bfloat16)
            pre_g = dot(g, w1e) + dot(belows[d][b], w1s) + dot(bottom, w1d)
            hid_g = jnp.maximum(pre_g, 0.0).astype(jnp.bfloat16)
            ghost = g.astype(jnp.float32) + layer_norm(dot(hid_g, w2))
            ghost = jnp.where(idx[2 + d] > 0, ghost, 0.0).astype(jnp.bfloat16)
            before = dot(down, fresh) + dot(t_down, ghost)
            total = total + fresh.astype(jnp.float32) + before
            e_out[d, b] = fresh
            g_out[d][b] = ghost
        pre = dot(h, n1[:width]) + dot(total.astype(jnp.bfloat16), n1[width:]) + temb_ref[...]
        hid = jnp.maximum(pre, 0.0).astype(jnp.bfloat16)
        h_new = (h.astype(jnp.float32) + layer_norm(dot(hid, n2))).astype(jnp.bfloat16)
        h_out[b] = h_new
        for d in range(3):
            bot, top = mats[6 * d][...], mats[6 * d + 1][...]
            bot_out[d][b] = dot(bot, h_new).astype(jnp.bfloat16)
            top_out[d][b] = dot(top, h_new).astype(jnp.bfloat16)


def whole(shape):
    return pl.BlockSpec(shape, lambda i, idx: (0,) * len(shape))


def run_layer(idx, h, e, ghosts, aboves, belows, temb, mine_all, other_all, scales, omask, mats):
    batch, rows, width = h.shape
    counts = [g.shape[1] for g in ghosts]
    out_shape = (
        [jax.ShapeDtypeStruct(h.shape, h.dtype), jax.ShapeDtypeStruct(e.shape, e.dtype)]
        + [jax.ShapeDtypeStruct(g.shape, g.dtype) for g in ghosts]
        + [jax.ShapeDtypeStruct((batch, c, width), h.dtype) for c in counts] * 2
    )
    flat_mats = [m for group in mats for m in group]
    layer_block = (1,) + mine_all.shape[1:]
    operands = [h, e, *ghosts, *aboves, *belows, temb]
    in_specs = [whole(x.shape) for x in operands]
    in_specs += [pl.BlockSpec(layer_block, lambda i, idx: (idx[0], 0, 0))] * 2
    tail = [scales, omask, *flat_mats]
    in_specs += [whole(x.shape) for x in tail]
    grid_spec = pltpu.PrefetchScalarGridSpec(
        num_scalar_prefetch=1,
        grid=(1,),
        in_specs=in_specs,
        out_specs=[whole(o.shape) for o in out_shape],
    )
    res = pl.pallas_call(
        layer_kernel,
        out_shape=out_shape,
        grid_spec=grid_spec,
        input_output_aliases={1: 0, 2: 1, 3: 2, 4: 3, 5: 4},
    )(idx, *operands, mine_all, other_all, *tail)
    return res[0], res[1], tuple(res[2:5]), tuple(res[5:8]), tuple(res[8:11])


def local(
    nodes_in,
    edges_in,
    codes,
    type_table,
    order,
    edge_w1,
    edge_w2,
    node_w1,
    node_w2,
    edge_v1,
    edge_v2,
    node_v1,
    node_v2,
):
    section_count = lax.axis_size("section")
    section_id = lax.axis_index("section")
    count_z = lax.axis_size("space") // 16
    space_id = lax.axis_index("space")
    coords = (space_id // (4 * count_z), space_id // count_z % 4, space_id % count_z)
    counts = (4, 4, count_z)
    strides = (4 * count_z, count_z, 1)
    width = nodes_in.shape[-1]
    local_count = nodes_in.shape[0]
    rows = nodes_in.shape[1]
    batches = local_count * section_count
    type_ids = lax.broadcasted_iota(jnp.int32, (codes.shape[0], type_table.shape[0]), 1)
    one_hot = (codes[:, None] == type_ids).astype(jnp.float32)
    type_embed = jnp.sum(one_hot[:, :, None] * type_table[None, :, :], axis=1)
    divisor = jnp.float32(batches + 2 * section_count)

    mine = section_id * local_count + jnp.arange(local_count, dtype=jnp.int32)
    slots = jnp.arange(batches, dtype=jnp.int32)
    position = jnp.sum(
        jnp.where(order[None, :] == mine[:, None], slots[None, :], 0), axis=1
    )

    core = space_id % 2
    sizes = [w.shape[1] for w in (edge_w1, edge_w2, node_w1, node_w2)]
    halves = (
        jnp.concatenate([edge_w1[0], edge_w2[0], node_w1[0], node_w2[0]], axis=0),
        jnp.concatenate([edge_v1[0], edge_v2[0], node_v1[0], node_v2[0]], axis=0),
    )
    own_half = jnp.where(core == 0, halves[0], halves[1])
    own_all = lax.all_gather(own_half, "section", axis=0, tiled=False)
    space_count = lax.axis_size("space")
    swap = [(i, i ^ 1) for i in range(space_count)]
    other_all = lax.ppermute(own_all, "space", swap)
    starts = [sum(sizes[:i]) for i in range(4)]

    shape = (BX, BY, BZ)
    mats = plane_mats(shape)
    grid_pos = np.stack(np.unravel_index(np.arange(rows), shape), axis=1)
    omask = jnp.stack(
        [
            jnp.broadcast_to(
                (coords[a] * shape[a] + grid_pos[:, a] < shape[a] * counts[a] - 1)[:, None],
                (rows, width),
            ).astype(jnp.float32)
            for a in range(3)
        ]
    )
    h0 = nodes_in
    e0 = jnp.transpose(edges_in, (1, 0, 2, 3))
    bot0 = tuple(jnp.einsum("pr,brw->bpw", mats[a][0], h0).astype(jnp.bfloat16) for a in range(3))
    top0 = tuple(jnp.einsum("pr,brw->bpw", mats[a][1], h0).astype(jnp.bfloat16) for a in range(3))
    ghosts0 = tuple(
        from_behind(
            jnp.einsum("pr,brw->bpw", mats[a][1], e0[a]).astype(jnp.bfloat16),
            "space",
            strides[a],
        )
        for a in range(3)
    )

    lower_flags = [(coords[a] > 0).astype(jnp.int32) for a in range(3)]

    def layer_step(layer_id, carry):
        h, e, ghosts, bots, tops = carry
        scales = (position + 2 * section_count - 2 - layer_id).astype(jnp.float32) / divisor
        scales = jnp.broadcast_to(scales[:, None], (local_count, width))
        idx = jnp.stack([layer_id, core] + lower_flags).astype(jnp.int32)
        aboves = tuple(from_behind(bots[a], "space", -strides[a]) for a in range(3))
        belows = tuple(from_behind(tops[a], "space", strides[a]) for a in range(3))
        return run_layer(
            idx, h, e, ghosts, aboves, belows, type_embed, own_all, other_all, scales, omask, mats
        )

    h, _, _, _, _ = lax.fori_loop(
        0, section_count, layer_step, (h0, e0, ghosts0, bot0, top0)
    )
    return h


def solution(mesh):
    return jax.shard_map(
        local,
        mesh=mesh,
        in_specs=(
            P("section", "space", None),
            P("section", None, "space", None),
            P("space"),
            P(),
            P(),
            P("section", None, None),
            P("section", None, None),
            P("section", None, None),
            P("section", None, None),
            P("section", None, None),
            P("section", None, None),
            P("section", None, None),
            P("section", None, None),
        ),
        out_specs=P("section", "space", None),
        check_vma=False,
    )
```

```python
import jax
import jax.numpy as jnp
from jax import lax
from jax.sharding import PartitionSpec as P
from jax.experimental import pallas as pl
from jax.experimental.pallas import tpu as pltpu
import numpy as np

BX = 8
BY = 4
BZ = 4


def from_behind(shard, axis, by):
    peers = lax.axis_size(axis)
    pairs = [(i, i + by) for i in range(peers) if 0 <= i + by < peers]
    return lax.ppermute(shard, axis, pairs)


def layer_norm(values):
    centre = jnp.mean(values, axis=-1, keepdims=True)
    spread = jnp.mean((values - centre) * (values - centre), axis=-1, keepdims=True)
    return (values - centre) * lax.rsqrt(spread + 1e-05)


def predict(weight, velocity, scales):
    return (
        weight.astype(jnp.float32)[None]
        + scales[:, None, None] * velocity.astype(jnp.float32)[None]
    ).astype(jnp.bfloat16)


def plane_mats(shape):
    rows = int(np.prod(shape))
    coords = np.stack(np.unravel_index(np.arange(rows), shape), axis=1)
    strides = [int(np.prod(shape[a + 1:])) for a in range(3)]
    out = []
    for a in range(3):
        length = shape[a]
        plane = np.cumsum(coords[:, a] == 0) - 1
        index = np.zeros(rows, np.int64)
        for edge in range(length):
            picked = np.nonzero(coords[:, a] == edge)[0]
            index[picked] = np.arange(picked.size)
        count = rows // length
        bot = np.zeros((count, rows), np.float32)
        top = np.zeros((count, rows), np.float32)
        up = np.zeros((rows, rows), np.float32)
        t_up = np.zeros((rows, count), np.float32)
        down = np.zeros((rows, rows), np.float32)
        t_down = np.zeros((rows, count), np.float32)
        for r in range(rows):
            c = coords[r, a]
            if c == 0:
                bot[index[r], r] = 1
                t_down[r, index[r]] = 1
            else:
                down[r, r - strides[a]] = 1
            if c == length - 1:
                top[index[r], r] = 1
                t_up[r, index[r]] = 1
            else:
                up[r, r + strides[a]] = 1
        out.append(
            tuple(jnp.asarray(m, jnp.bfloat16) for m in (bot, top, up, t_up, down, t_down))
        )
    return out


def dot(a, b):
    return jnp.dot(a, b, preferred_element_type=jnp.float32)


def layer_kernel(*refs):
    idx = refs[0]
    (h_ref, e_ref, g0, g1, g2, a0, a1, a2, b0, b1, b2, temb_ref, mine_ref, other_ref, scale_ref,
     omask_ref) = refs[1:17]
    mats = refs[17:35]
    outs = refs[35:]
    h_out, e_out = outs[0], outs[1]
    g_out = outs[2:5]
    bot_out = outs[5:8]
    top_out = outs[8:11]
    ghosts = (g0, g1, g2)
    aboves = (a0, a1, a2)
    belows = (b0, b1, b2)
    width = h_ref.shape[-1]
    sizes = (3 * width, width, 2 * width, width)
    starts = [sum(sizes[:i]) for i in range(4)]
    core_zero = idx[1] == 0
    mine = mine_ref[0]
    other = other_ref[0]
    w_all = jnp.where(core_zero, mine, other).astype(jnp.float32)
    v_all = jnp.where(core_zero, other, mine).astype(jnp.float32)
    for b in range(h_ref.shape[0]):
        scale = scale_ref[b:b + 1, :]
        pred = (w_all + scale * v_all).astype(jnp.bfloat16)
        w1, w2, n1, n2 = (pred[starts[i]:starts[i] + sizes[i]] for i in range(4))
        h = h_ref[b]
        w1e, w1s, w1d = w1[:width], w1[width:2 * width], w1[2 * width:]
        h_src = dot(h, w1s)
        total = jnp.zeros(h.shape, jnp.float32)
        for d in range(3):
            bot, top, up, t_up, down, t_down = (m[...] for m in mats[6 * d:6 * d + 6])
            e = e_ref[d, b]
            nxt = (dot(up, h) + dot(t_up, aboves[d][b])).astype(jnp.bfloat16)
            pre = dot(e, w1e) + h_src + dot(nxt, w1d)
            hid = jnp.maximum(pre, 0.0).astype(jnp.bfloat16)
            fresh = e.astype(jnp.float32) + layer_norm(dot(hid, w2))
            fresh = jnp.where(omask_ref[d] > 0.5, fresh, 0.0).astype(jnp.bfloat16)
            g = ghosts[d][b]
            bottom = dot(bot, h).astype(jnp.bfloat16)
            pre_g = dot(g, w1e) + dot(belows[d][b], w1s) + dot(bottom, w1d)
            hid_g = jnp.maximum(pre_g, 0.0).astype(jnp.bfloat16)
            ghost = g.astype(jnp.float32) + layer_norm(dot(hid_g, w2))
            ghost = jnp.where(idx[2 + d] > 0, ghost, 0.0).astype(jnp.bfloat16)
            before = dot(down, fresh) + dot(t_down, ghost)
            total = total + fresh.astype(jnp.float32) + before
            e_out[d, b] = fresh
            g_out[d][b] = ghost
        pre = dot(h, n1[:width]) + dot(total.astype(jnp.bfloat16), n1[width:]) + temb_ref[...]
        hid = jnp.maximum(pre, 0.0).astype(jnp.bfloat16)
        h_new = (h.astype(jnp.float32) + layer_norm(dot(hid, n2))).astype(jnp.bfloat16)
        h_out[b] = h_new
        for d in range(3):
            bot, top = mats[6 * d][...], mats[6 * d + 1][...]
            bot_out[d][b] = dot(bot, h_new).astype(jnp.bfloat16)
            top_out[d][b] = dot(top, h_new).astype(jnp.bfloat16)


def whole(shape):
    return pl.BlockSpec(shape, lambda i, idx: (0,) * len(shape))


def run_layer(idx, h, e, ghosts, aboves, belows, temb, mine_all, other_all, scales, omask, mats):
    batch, rows, width = h.shape
    counts = [g.shape[1] for g in ghosts]
    out_shape = (
        [jax.ShapeDtypeStruct(h.shape, h.dtype), jax.ShapeDtypeStruct(e.shape, e.dtype)]
        + [jax.ShapeDtypeStruct(g.shape, g.dtype) for g in ghosts]
        + [jax.ShapeDtypeStruct((batch, c, width), h.dtype) for c in counts] * 2
    )
    flat_mats = [m for group in mats for m in group]
    layer_block = (1,) + mine_all.shape[1:]
    operands = [h, e, *ghosts, *aboves, *belows, temb]
    in_specs = [whole(x.shape) for x in operands]
    in_specs += [pl.BlockSpec(layer_block, lambda i, idx: (idx[0], 0, 0))] * 2
    tail = [scales, omask, *flat_mats]
    in_specs += [whole(x.shape) for x in tail]
    grid_spec = pltpu.PrefetchScalarGridSpec(
        num_scalar_prefetch=1,
        grid=(1,),
        in_specs=in_specs,
        out_specs=[whole(o.shape) for o in out_shape],
    )
    res = pl.pallas_call(
        layer_kernel,
        out_shape=out_shape,
        grid_spec=grid_spec,
        input_output_aliases={1: 0, 2: 1, 3: 2, 4: 3, 5: 4},
    )(idx, *operands, mine_all, other_all, *tail)
    return res[0], res[1], tuple(res[2:5]), tuple(res[5:8]), tuple(res[8:11])


def local(
    nodes_in,
    edges_in,
    codes,
    type_table,
    order,
    edge_w1,
    edge_w2,
    node_w1,
    node_w2,
    edge_v1,
    edge_v2,
    node_v1,
    node_v2,
):
    section_count = lax.axis_size("section")
    section_id = lax.axis_index("section")
    count_z = lax.axis_size("space") // 16
    space_id = lax.axis_index("space")
    coords = (space_id // (4 * count_z), space_id // count_z % 4, space_id % count_z)
    counts = (4, 4, count_z)
    strides = (4 * count_z, count_z, 1)
    width = nodes_in.shape[-1]
    local_count = nodes_in.shape[0]
    rows = nodes_in.shape[1]
    batches = local_count * section_count
    type_ids = lax.broadcasted_iota(jnp.int32, (codes.shape[0], type_table.shape[0]), 1)
    one_hot = (codes[:, None] == type_ids).astype(jnp.float32)
    type_embed = jnp.sum(one_hot[:, :, None] * type_table[None, :, :], axis=1)
    divisor = jnp.float32(batches + 2 * section_count)

    mine = section_id * local_count + jnp.arange(local_count, dtype=jnp.int32)
    slots = jnp.arange(batches, dtype=jnp.int32)
    position = jnp.sum(
        jnp.where(order[None, :] == mine[:, None], slots[None, :], 0), axis=1
    )

    core = space_id % 2
    sizes = [w.shape[1] for w in (edge_w1, edge_w2, node_w1, node_w2)]
    halves = (
        jnp.concatenate([edge_w1[0], edge_w2[0], node_w1[0], node_w2[0]], axis=0),
        jnp.concatenate([edge_v1[0], edge_v2[0], node_v1[0], node_v2[0]], axis=0),
    )
    own_half = jnp.where(core == 0, halves[0], halves[1])
    space_count = lax.axis_size("space")
    ring = 4
    ring_stride = space_count // ring
    ring_pos = coords[0]
    chunk = own_half.shape[0] // ring
    my_part = lax.dynamic_slice_in_dim(own_half, ring_pos * chunk, chunk, axis=0)
    got = [lax.all_gather(my_part, "section", axis=0, tiled=False)]
    for k in range(1, ring):
        shift = [(i, (i + k * ring_stride) % space_count) for i in range(space_count)]
        got.append(lax.ppermute(got[0], "space", shift))
    stacked = jnp.stack(got)
    which = (ring_pos - jnp.arange(ring, dtype=jnp.int32)) % ring
    own_all = jnp.take(stacked, which, axis=0)
    own_all = jnp.transpose(own_all, (1, 0, 2, 3)).reshape(
        (section_count, ring * chunk, own_half.shape[1])
    )
    swap = [(i, i ^ 1) for i in range(space_count)]
    other_all = lax.ppermute(own_all, "space", swap)
    starts = [sum(sizes[:i]) for i in range(4)]

    shape = (BX, BY, BZ)
    mats = plane_mats(shape)
    grid_pos = np.stack(np.unravel_index(np.arange(rows), shape), axis=1)
    omask = jnp.stack(
        [
            jnp.broadcast_to(
                (coords[a] * shape[a] + grid_pos[:, a] < shape[a] * counts[a] - 1)[:, None],
                (rows, width),
            ).astype(jnp.float32)
            for a in range(3)
        ]
    )
    h0 = nodes_in
    e0 = jnp.transpose(edges_in, (1, 0, 2, 3))
    bot0 = tuple(jnp.einsum("pr,brw->bpw", mats[a][0], h0).astype(jnp.bfloat16) for a in range(3))
    top0 = tuple(jnp.einsum("pr,brw->bpw", mats[a][1], h0).astype(jnp.bfloat16) for a in range(3))
    ghosts0 = tuple(
        from_behind(
            jnp.einsum("pr,brw->bpw", mats[a][1], e0[a]).astype(jnp.bfloat16),
            "space",
            strides[a],
        )
        for a in range(3)
    )

    lower_flags = [(coords[a] > 0).astype(jnp.int32) for a in range(3)]

    def layer_step(layer_id, carry):
        h, e, ghosts, bots, tops = carry
        scales = (position + 2 * section_count - 2 - layer_id).astype(jnp.float32) / divisor
        scales = jnp.broadcast_to(scales[:, None], (local_count, width))
        idx = jnp.stack([layer_id, core] + lower_flags).astype(jnp.int32)
        aboves = tuple(from_behind(bots[a], "space", -strides[a]) for a in range(3))
        belows = tuple(from_behind(tops[a], "space", strides[a]) for a in range(3))
        return run_layer(
            idx, h, e, ghosts, aboves, belows, type_embed, own_all, other_all, scales, omask, mats
        )

    h, _, _, _, _ = lax.fori_loop(
        0, section_count, layer_step, (h0, e0, ghosts0, bot0, top0)
    )
    return h


def solution(mesh):
    return jax.shard_map(
        local,
        mesh=mesh,
        in_specs=(
            P("section", "space", None),
            P("section", None, "space", None),
            P("space"),
            P(),
            P(),
            P("section", None, None),
            P("section", None, None),
            P("section", None, None),
            P("section", None, None),
            P("section", None, None),
            P("section", None, None),
            P("section", None, None),
            P("section", None, None),
        ),
        out_specs=P("section", "space", None),
        check_vma=False,
    )
```

```python
import jax
import jax.numpy as jnp
from jax import lax
from jax.sharding import PartitionSpec as P
from jax.experimental import pallas as pl
from jax.experimental.pallas import tpu as pltpu
import numpy as np

BX = 8
BY = 4
BZ = 4


def from_behind(shard, axis, by):
    peers = lax.axis_size(axis)
    pairs = [(i, i + by) for i in range(peers) if 0 <= i + by < peers]
    return lax.ppermute(shard, axis, pairs)


def along_line(shard, by, stride, count):
    peers = lax.axis_size("space")
    step = by // stride
    pairs = [
        (i, i + by) for i in range(peers) if 0 <= (i // stride) % count + step < count
    ]
    return lax.ppermute(shard, "space", pairs)


def layer_norm(values):
    centre = jnp.mean(values, axis=-1, keepdims=True)
    spread = jnp.mean((values - centre) * (values - centre), axis=-1, keepdims=True)
    return (values - centre) * lax.rsqrt(spread + 1e-05)


def predict(weight, velocity, scales):
    return (
        weight.astype(jnp.float32)[None]
        + scales[:, None, None] * velocity.astype(jnp.float32)[None]
    ).astype(jnp.bfloat16)


def plane_mats(shape):
    rows = int(np.prod(shape))
    coords = np.stack(np.unravel_index(np.arange(rows), shape), axis=1)
    strides = [int(np.prod(shape[a + 1:])) for a in range(3)]
    out = []
    for a in range(3):
        length = shape[a]
        plane = np.cumsum(coords[:, a] == 0) - 1
        index = np.zeros(rows, np.int64)
        for edge in range(length):
            picked = np.nonzero(coords[:, a] == edge)[0]
            index[picked] = np.arange(picked.size)
        count = rows // length
        bot = np.zeros((count, rows), np.float32)
        top = np.zeros((count, rows), np.float32)
        up = np.zeros((rows, rows), np.float32)
        t_up = np.zeros((rows, count), np.float32)
        down = np.zeros((rows, rows), np.float32)
        t_down = np.zeros((rows, count), np.float32)
        for r in range(rows):
            c = coords[r, a]
            if c == 0:
                bot[index[r], r] = 1
                t_down[r, index[r]] = 1
            else:
                down[r, r - strides[a]] = 1
            if c == length - 1:
                top[index[r], r] = 1
                t_up[r, index[r]] = 1
            else:
                up[r, r + strides[a]] = 1
        out.append(
            tuple(jnp.asarray(m, jnp.bfloat16) for m in (bot, top, up, t_up, down, t_down))
        )
    return out


def dot(a, b):
    return jnp.dot(a, b, preferred_element_type=jnp.float32)


def layer_kernel(*refs):
    idx = refs[0]
    (h_ref, e_ref, g0, g1, g2, a0, a1, a2, b0, b1, b2, temb_ref, mine_ref, other_ref, scale_ref,
     omask_ref) = refs[1:17]
    mats = refs[17:35]
    outs = refs[35:]
    h_out, e_out = outs[0], outs[1]
    g_out = outs[2:5]
    bot_out = outs[5:8]
    top_out = outs[8:11]
    ghosts = (g0, g1, g2)
    aboves = (a0, a1, a2)
    belows = (b0, b1, b2)
    width = h_ref.shape[-1]
    sizes = (3 * width, width, 2 * width, width)
    starts = [sum(sizes[:i]) for i in range(4)]
    core_zero = idx[1] == 0
    mine = mine_ref[0]
    other = other_ref[0]
    w_all = jnp.where(core_zero, mine, other).astype(jnp.float32)
    v_all = jnp.where(core_zero, other, mine).astype(jnp.float32)
    for b in range(h_ref.shape[0]):
        scale = scale_ref[b:b + 1, :]
        pred = (w_all + scale * v_all).astype(jnp.bfloat16)
        w1, w2, n1, n2 = (pred[starts[i]:starts[i] + sizes[i]] for i in range(4))
        h = h_ref[b]
        w1e, w1s, w1d = w1[:width], w1[width:2 * width], w1[2 * width:]
        h_src = dot(h, w1s)
        total = jnp.zeros(h.shape, jnp.float32)
        for d in range(3):
            bot, top, up, t_up, down, t_down = (m[...] for m in mats[6 * d:6 * d + 6])
            e = e_ref[d, b]
            nxt = (dot(up, h) + dot(t_up, aboves[d][b])).astype(jnp.bfloat16)
            pre = dot(e, w1e) + h_src + dot(nxt, w1d)
            hid = jnp.maximum(pre, 0.0).astype(jnp.bfloat16)
            fresh = e.astype(jnp.float32) + layer_norm(dot(hid, w2))
            fresh = jnp.where(omask_ref[d] > 0.5, fresh, 0.0).astype(jnp.bfloat16)
            g = ghosts[d][b]
            bottom = dot(bot, h).astype(jnp.bfloat16)
            pre_g = dot(g, w1e) + dot(belows[d][b], w1s) + dot(bottom, w1d)
            hid_g = jnp.maximum(pre_g, 0.0).astype(jnp.bfloat16)
            ghost = g.astype(jnp.float32) + layer_norm(dot(hid_g, w2))
            ghost = jnp.where(idx[2 + d] > 0, ghost, 0.0).astype(jnp.bfloat16)
            before = dot(down, fresh) + dot(t_down, ghost)
            total = total + fresh.astype(jnp.float32) + before
            e_out[d, b] = fresh
            g_out[d][b] = ghost
        pre = dot(h, n1[:width]) + dot(total.astype(jnp.bfloat16), n1[width:]) + temb_ref[...]
        hid = jnp.maximum(pre, 0.0).astype(jnp.bfloat16)
        h_new = (h.astype(jnp.float32) + layer_norm(dot(hid, n2))).astype(jnp.bfloat16)
        h_out[b] = h_new
        for d in range(3):
            bot, top = mats[6 * d][...], mats[6 * d + 1][...]
            bot_out[d][b] = dot(bot, h_new).astype(jnp.bfloat16)
            top_out[d][b] = dot(top, h_new).astype(jnp.bfloat16)


def whole(shape):
    return pl.BlockSpec(shape, lambda i, idx: (0,) * len(shape))


def run_layer(idx, h, e, ghosts, aboves, belows, temb, mine_all, other_all, scales, omask, mats):
    batch, rows, width = h.shape
    counts = [g.shape[1] for g in ghosts]
    out_shape = (
        [jax.ShapeDtypeStruct(h.shape, h.dtype), jax.ShapeDtypeStruct(e.shape, e.dtype)]
        + [jax.ShapeDtypeStruct(g.shape, g.dtype) for g in ghosts]
        + [jax.ShapeDtypeStruct((batch, c, width), h.dtype) for c in counts] * 2
    )
    flat_mats = [m for group in mats for m in group]
    layer_block = (1,) + mine_all.shape[1:]
    operands = [h, e, *ghosts, *aboves, *belows, temb]
    in_specs = [whole(x.shape) for x in operands]
    in_specs += [pl.BlockSpec(layer_block, lambda i, idx: (idx[0], 0, 0))] * 2
    tail = [scales, omask, *flat_mats]
    in_specs += [whole(x.shape) for x in tail]
    grid_spec = pltpu.PrefetchScalarGridSpec(
        num_scalar_prefetch=1,
        grid=(1,),
        in_specs=in_specs,
        out_specs=[whole(o.shape) for o in out_shape],
    )
    res = pl.pallas_call(
        layer_kernel,
        out_shape=out_shape,
        grid_spec=grid_spec,
        input_output_aliases={1: 0, 2: 1, 3: 2, 4: 3, 5: 4},
    )(idx, *operands, mine_all, other_all, *tail)
    return res[0], res[1], tuple(res[2:5]), tuple(res[5:8]), tuple(res[8:11])


def local(
    nodes_in,
    edges_in,
    codes,
    type_table,
    order,
    edge_w1,
    edge_w2,
    node_w1,
    node_w2,
    edge_v1,
    edge_v2,
    node_v1,
    node_v2,
):
    section_count = lax.axis_size("section")
    section_id = lax.axis_index("section")
    count_z = lax.axis_size("space") // 16
    space_id = lax.axis_index("space")
    coords = (space_id // (4 * count_z), space_id // count_z % 4, space_id % count_z)
    counts = (4, 4, count_z)
    strides = (4 * count_z, count_z, 1)
    width = nodes_in.shape[-1]
    local_count = nodes_in.shape[0]
    rows = nodes_in.shape[1]
    batches = local_count * section_count
    type_ids = lax.broadcasted_iota(jnp.int32, (codes.shape[0], type_table.shape[0]), 1)
    one_hot = (codes[:, None] == type_ids).astype(jnp.float32)
    type_embed = jnp.sum(one_hot[:, :, None] * type_table[None, :, :], axis=1)
    divisor = jnp.float32(batches + 2 * section_count)

    mine = section_id * local_count + jnp.arange(local_count, dtype=jnp.int32)
    slots = jnp.arange(batches, dtype=jnp.int32)
    position = jnp.sum(
        jnp.where(order[None, :] == mine[:, None], slots[None, :], 0), axis=1
    )

    core = space_id % 2
    sizes = [w.shape[1] for w in (edge_w1, edge_w2, node_w1, node_w2)]
    halves = (
        jnp.concatenate([edge_w1[0], edge_w2[0], node_w1[0], node_w2[0]], axis=0),
        jnp.concatenate([edge_v1[0], edge_v2[0], node_v1[0], node_v2[0]], axis=0),
    )
    own_half = jnp.where(core == 0, halves[0], halves[1])
    space_count = lax.axis_size("space")
    ring = 4
    ring_stride = space_count // ring
    ring_pos = coords[0]
    chunk = own_half.shape[0] // ring
    my_part = lax.dynamic_slice_in_dim(own_half, ring_pos * chunk, chunk, axis=0)
    got = [lax.all_gather(my_part, "section", axis=0, tiled=False)]
    for k in range(1, ring):
        shift = [(i, (i + k * ring_stride) % space_count) for i in range(space_count)]
        got.append(lax.ppermute(got[0], "space", shift))
    own_all = jnp.zeros((section_count, ring * chunk, own_half.shape[1]), own_half.dtype)
    for k in range(ring):
        own_all = lax.dynamic_update_slice_in_dim(
            own_all, got[k], (ring_pos - k) % ring * chunk, axis=1
        )
    swap = [(i, i ^ 1) for i in range(space_count)]
    other_all = lax.ppermute(own_all, "space", swap)
    starts = [sum(sizes[:i]) for i in range(4)]

    shape = (BX, BY, BZ)
    mats = plane_mats(shape)
    grid_pos = np.stack(np.unravel_index(np.arange(rows), shape), axis=1)
    omask = jnp.stack(
        [
            jnp.broadcast_to(
                (coords[a] * shape[a] + grid_pos[:, a] < shape[a] * counts[a] - 1)[:, None],
                (rows, width),
            ).astype(jnp.float32)
            for a in range(3)
        ]
    )
    h0 = nodes_in
    e0 = jnp.transpose(edges_in, (1, 0, 2, 3))
    bot0 = tuple(jnp.einsum("pr,brw->bpw", mats[a][0], h0).astype(jnp.bfloat16) for a in range(3))
    top0 = tuple(jnp.einsum("pr,brw->bpw", mats[a][1], h0).astype(jnp.bfloat16) for a in range(3))
    ghosts0 = tuple(
        along_line(
            jnp.einsum("pr,brw->bpw", mats[a][1], e0[a]).astype(jnp.bfloat16),
            strides[a],
            strides[a],
            counts[a],
        )
        for a in range(3)
    )

    lower_flags = [(coords[a] > 0).astype(jnp.int32) for a in range(3)]

    def layer_step(layer_id, carry):
        h, e, ghosts, bots, tops = carry
        scales = (position + 2 * section_count - 2 - layer_id).astype(jnp.float32) / divisor
        scales = jnp.broadcast_to(scales[:, None], (local_count, width))
        idx = jnp.stack([layer_id, core] + lower_flags).astype(jnp.int32)
        aboves = tuple(along_line(bots[a], -strides[a], strides[a], counts[a]) for a in range(3))
        belows = tuple(along_line(tops[a], strides[a], strides[a], counts[a]) for a in range(3))
        return run_layer(
            idx, h, e, ghosts, aboves, belows, type_embed, own_all, other_all, scales, omask, mats
        )

    h, _, _, _, _ = lax.fori_loop(
        0, section_count, layer_step, (h0, e0, ghosts0, bot0, top0)
    )
    return h


def solution(mesh):
    return jax.shard_map(
        local,
        mesh=mesh,
        in_specs=(
            P("section", "space", None),
            P("section", None, "space", None),
            P("space"),
            P(),
            P(),
            P("section", None, None),
            P("section", None, None),
            P("section", None, None),
            P("section", None, None),
            P("section", None, None),
            P("section", None, None),
            P("section", None, None),
            P("section", None, None),
        ),
        out_specs=P("section", "space", None),
        check_vma=False,
    )
```

```python
import jax
import jax.numpy as jnp
from jax import lax
from jax.sharding import PartitionSpec as P
from jax.experimental import pallas as pl
from jax.experimental.pallas import tpu as pltpu
import numpy as np

BX = 8
BY = 4
BZ = 4


def from_behind(shard, axis, by):
    peers = lax.axis_size(axis)
    pairs = [(i, i + by) for i in range(peers) if 0 <= i + by < peers]
    return lax.ppermute(shard, axis, pairs)


def along_line(shard, by, stride, count):
    peers = lax.axis_size("space")
    step = by // stride
    pairs = [
        (i, i + by) for i in range(peers) if 0 <= (i // stride) % count + step < count
    ]
    return lax.ppermute(shard, "space", pairs)


def layer_norm(values):
    centre = jnp.mean(values, axis=-1, keepdims=True)
    spread = jnp.mean((values - centre) * (values - centre), axis=-1, keepdims=True)
    return (values - centre) * lax.rsqrt(spread + 1e-05)


def predict(weight, velocity, scales):
    return (
        weight.astype(jnp.float32)[None]
        + scales[:, None, None] * velocity.astype(jnp.float32)[None]
    ).astype(jnp.bfloat16)


def plane_mats(shape):
    rows = int(np.prod(shape))
    coords = np.stack(np.unravel_index(np.arange(rows), shape), axis=1)
    strides = [int(np.prod(shape[a + 1:])) for a in range(3)]
    out = []
    for a in range(3):
        length = shape[a]
        plane = np.cumsum(coords[:, a] == 0) - 1
        index = np.zeros(rows, np.int64)
        for edge in range(length):
            picked = np.nonzero(coords[:, a] == edge)[0]
            index[picked] = np.arange(picked.size)
        count = rows // length
        bot = np.zeros((count, rows), np.float32)
        top = np.zeros((count, rows), np.float32)
        up = np.zeros((rows, rows), np.float32)
        t_up = np.zeros((rows, count), np.float32)
        down = np.zeros((rows, rows), np.float32)
        t_down = np.zeros((rows, count), np.float32)
        for r in range(rows):
            c = coords[r, a]
            if c == 0:
                bot[index[r], r] = 1
                t_down[r, index[r]] = 1
            else:
                down[r, r - strides[a]] = 1
            if c == length - 1:
                top[index[r], r] = 1
                t_up[r, index[r]] = 1
            else:
                up[r, r + strides[a]] = 1
        out.append(
            tuple(jnp.asarray(m, jnp.bfloat16) for m in (bot, top, up, t_up, down, t_down))
        )
    return out


def dot(a, b):
    return jnp.dot(a, b, preferred_element_type=jnp.float32)


def layer_kernel(*refs):
    idx = refs[0]
    (h_ref, e_ref, g0, g1, g2, a0, a1, a2, b0, b1, b2, temb_ref, mine_ref, other_ref, scale_ref,
     omask_ref) = refs[1:17]
    mats = refs[17:35]
    outs = refs[35:]
    h_out, e_out = outs[0], outs[1]
    g_out = outs[2:5]
    bot_out = outs[5:8]
    top_out = outs[8:11]
    ghosts = (g0, g1, g2)
    aboves = (a0, a1, a2)
    belows = (b0, b1, b2)
    width = h_ref.shape[-1]
    sizes = (3 * width, width, 2 * width, width)
    starts = [sum(sizes[:i]) for i in range(4)]
    core_zero = idx[1] == 0
    mine = mine_ref[0]
    other = other_ref[0]
    w_all = jnp.where(core_zero, mine, other).astype(jnp.float32)
    v_all = jnp.where(core_zero, other, mine).astype(jnp.float32)
    for b in range(h_ref.shape[0]):
        scale = scale_ref[b:b + 1, :]
        pred = (w_all + scale * v_all).astype(jnp.bfloat16)
        w1, w2, n1, n2 = (pred[starts[i]:starts[i] + sizes[i]] for i in range(4))
        h = h_ref[b]
        w1e, w1s, w1d = w1[:width], w1[width:2 * width], w1[2 * width:]
        h_src = dot(h, w1s)
        total = jnp.zeros(h.shape, jnp.float32)
        for d in range(3):
            bot, top, up, t_up, down, t_down = (m[...] for m in mats[6 * d:6 * d + 6])
            e = e_ref[d, b]
            nxt = (dot(up, h) + dot(t_up, aboves[d][b])).astype(jnp.bfloat16)
            pre = dot(e, w1e) + h_src + dot(nxt, w1d)
            hid = jnp.maximum(pre, 0.0).astype(jnp.bfloat16)
            fresh = e.astype(jnp.float32) + layer_norm(dot(hid, w2))
            fresh = jnp.where(omask_ref[d] > 0.5, fresh, 0.0).astype(jnp.bfloat16)
            g = ghosts[d][b]
            bottom = dot(bot, h).astype(jnp.bfloat16)
            pre_g = dot(g, w1e) + dot(belows[d][b], w1s) + dot(bottom, w1d)
            hid_g = jnp.maximum(pre_g, 0.0).astype(jnp.bfloat16)
            ghost = g.astype(jnp.float32) + layer_norm(dot(hid_g, w2))
            ghost = jnp.where(idx[2 + d] > 0, ghost, 0.0).astype(jnp.bfloat16)
            before = dot(down, fresh) + dot(t_down, ghost)
            total = total + fresh.astype(jnp.float32) + before
            e_out[d, b] = fresh
            g_out[d][b] = ghost
        pre = dot(h, n1[:width]) + dot(total.astype(jnp.bfloat16), n1[width:]) + temb_ref[...]
        hid = jnp.maximum(pre, 0.0).astype(jnp.bfloat16)
        h_new = (h.astype(jnp.float32) + layer_norm(dot(hid, n2))).astype(jnp.bfloat16)
        h_out[b] = h_new
        for d in range(3):
            bot, top = mats[6 * d][...], mats[6 * d + 1][...]
            bot_out[d][b] = dot(bot, h_new).astype(jnp.bfloat16)
            top_out[d][b] = dot(top, h_new).astype(jnp.bfloat16)


def whole(shape):
    return pl.BlockSpec(shape, lambda i, idx: (0,) * len(shape))


def run_layer(idx, h, e, ghosts, aboves, belows, temb, mine_all, other_all, scales, omask, mats):
    batch, rows, width = h.shape
    counts = [g.shape[1] for g in ghosts]
    out_shape = (
        [jax.ShapeDtypeStruct(h.shape, h.dtype), jax.ShapeDtypeStruct(e.shape, e.dtype)]
        + [jax.ShapeDtypeStruct(g.shape, g.dtype) for g in ghosts]
        + [jax.ShapeDtypeStruct((batch, c, width), h.dtype) for c in counts] * 2
    )
    flat_mats = [m for group in mats for m in group]
    layer_block = (1,) + mine_all.shape[1:]
    operands = [h, e, *ghosts, *aboves, *belows, temb]
    in_specs = [whole(x.shape) for x in operands]
    in_specs += [pl.BlockSpec(layer_block, lambda i, idx: (idx[0], 0, 0))] * 2
    tail = [scales, omask, *flat_mats]
    in_specs += [whole(x.shape) for x in tail]
    grid_spec = pltpu.PrefetchScalarGridSpec(
        num_scalar_prefetch=1,
        grid=(1,),
        in_specs=in_specs,
        out_specs=[whole(o.shape) for o in out_shape],
    )
    res = pl.pallas_call(
        layer_kernel,
        out_shape=out_shape,
        grid_spec=grid_spec,
        input_output_aliases={1: 0, 2: 1, 3: 2, 4: 3, 5: 4},
    )(idx, *operands, mine_all, other_all, *tail)
    return res[0], res[1], tuple(res[2:5]), tuple(res[5:8]), tuple(res[8:11])


def local(
    nodes_in,
    edges_in,
    codes,
    type_table,
    order,
    edge_w1,
    edge_w2,
    node_w1,
    node_w2,
    edge_v1,
    edge_v2,
    node_v1,
    node_v2,
):
    section_count = lax.axis_size("section")
    section_id = lax.axis_index("section")
    count_z = lax.axis_size("space") // 16
    space_id = lax.axis_index("space")
    coords = (space_id // (4 * count_z), space_id // count_z % 4, space_id % count_z)
    counts = (4, 4, count_z)
    strides = (4 * count_z, count_z, 1)
    width = nodes_in.shape[-1]
    local_count = nodes_in.shape[0]
    rows = nodes_in.shape[1]
    batches = local_count * section_count
    type_ids = lax.broadcasted_iota(jnp.int32, (codes.shape[0], type_table.shape[0]), 1)
    one_hot = (codes[:, None] == type_ids).astype(jnp.float32)
    type_embed = jnp.sum(one_hot[:, :, None] * type_table[None, :, :], axis=1)
    divisor = jnp.float32(batches + 2 * section_count)

    mine = section_id * local_count + jnp.arange(local_count, dtype=jnp.int32)
    slots = jnp.arange(batches, dtype=jnp.int32)
    position = jnp.sum(
        jnp.where(order[None, :] == mine[:, None], slots[None, :], 0), axis=1
    )

    core = space_id % 2
    sizes = [w.shape[1] for w in (edge_w1, edge_w2, node_w1, node_w2)]
    halves = (
        jnp.concatenate([edge_w1[0], edge_w2[0], node_w1[0], node_w2[0]], axis=0),
        jnp.concatenate([edge_v1[0], edge_v2[0], node_v1[0], node_v2[0]], axis=0),
    )
    own_half = jnp.where(core == 0, halves[0], halves[1])
    space_count = lax.axis_size("space")
    ring = 4
    ring_stride = space_count // ring
    ring_pos = coords[0]
    chunk = own_half.shape[0] // ring
    my_part = lax.dynamic_slice_in_dim(own_half, ring_pos * chunk, chunk, axis=0)
    layers = jnp.zeros((section_count,) + my_part.shape, my_part.dtype)
    layers = lax.dynamic_update_slice_in_dim(layers, my_part[None], section_id, axis=0)
    for k in range(1, section_count):
        shift = [(i, (i + k) % section_count) for i in range(section_count)]
        layers = lax.dynamic_update_slice_in_dim(
            layers,
            lax.ppermute(my_part, "section", shift)[None],
            (section_id - k) % section_count,
            axis=0,
        )
    got = [layers]
    for k in range(1, ring):
        shift = [(i, (i + k * ring_stride) % space_count) for i in range(space_count)]
        got.append(lax.ppermute(got[0], "space", shift))
    own_all = jnp.zeros((section_count, ring * chunk, own_half.shape[1]), own_half.dtype)
    for k in range(ring):
        own_all = lax.dynamic_update_slice_in_dim(
            own_all, got[k], (ring_pos - k) % ring * chunk, axis=1
        )
    swap = [(i, i ^ 1) for i in range(space_count)]
    other_all = lax.ppermute(own_all, "space", swap)
    starts = [sum(sizes[:i]) for i in range(4)]

    shape = (BX, BY, BZ)
    mats = plane_mats(shape)
    grid_pos = np.stack(np.unravel_index(np.arange(rows), shape), axis=1)
    omask = jnp.stack(
        [
            jnp.broadcast_to(
                (coords[a] * shape[a] + grid_pos[:, a] < shape[a] * counts[a] - 1)[:, None],
                (rows, width),
            ).astype(jnp.float32)
            for a in range(3)
        ]
    )
    h0 = nodes_in
    e0 = jnp.transpose(edges_in, (1, 0, 2, 3))
    bot0 = tuple(jnp.einsum("pr,brw->bpw", mats[a][0], h0).astype(jnp.bfloat16) for a in range(3))
    top0 = tuple(jnp.einsum("pr,brw->bpw", mats[a][1], h0).astype(jnp.bfloat16) for a in range(3))
    ghosts0 = tuple(
        along_line(
            jnp.einsum("pr,brw->bpw", mats[a][1], e0[a]).astype(jnp.bfloat16),
            strides[a],
            strides[a],
            counts[a],
        )
        for a in range(3)
    )

    lower_flags = [(coords[a] > 0).astype(jnp.int32) for a in range(3)]

    def layer_step(layer_id, carry):
        h, e, ghosts, bots, tops = carry
        scales = (position + 2 * section_count - 2 - layer_id).astype(jnp.float32) / divisor
        scales = jnp.broadcast_to(scales[:, None], (local_count, width))
        idx = jnp.stack([layer_id, core] + lower_flags).astype(jnp.int32)
        aboves = tuple(along_line(bots[a], -strides[a], strides[a], counts[a]) for a in range(3))
        belows = tuple(along_line(tops[a], strides[a], strides[a], counts[a]) for a in range(3))
        return run_layer(
            idx, h, e, ghosts, aboves, belows, type_embed, own_all, other_all, scales, omask, mats
        )

    h, _, _, _, _ = lax.fori_loop(
        0, section_count, layer_step, (h0, e0, ghosts0, bot0, top0)
    )
    return h


def solution(mesh):
    return jax.shard_map(
        local,
        mesh=mesh,
        in_specs=(
            P("section", "space", None),
            P("section", None, "space", None),
            P("space"),
            P(),
            P(),
            P("section", None, None),
            P("section", None, None),
            P("section", None, None),
            P("section", None, None),
            P("section", None, None),
            P("section", None, None),
            P("section", None, None),
            P("section", None, None),
        ),
        out_specs=P("section", "space", None),
        check_vma=False,
    )
```

```python
import jax
import jax.numpy as jnp
from jax import lax
from jax.sharding import PartitionSpec as P
from jax.experimental import pallas as pl
from jax.experimental.pallas import tpu as pltpu
import numpy as np

BX = 8
BY = 4
BZ = 4


def from_behind(shard, axis, by):
    peers = lax.axis_size(axis)
    pairs = [(i, i + by) for i in range(peers) if 0 <= i + by < peers]
    return lax.ppermute(shard, axis, pairs)


def along_line(shard, by, stride, count):
    peers = lax.axis_size("space")
    step = by // stride
    pairs = [
        (i, i + by) for i in range(peers) if 0 <= (i // stride) % count + step < count
    ]
    return lax.ppermute(shard, "space", pairs)


def layer_norm(values):
    centre = jnp.mean(values, axis=-1, keepdims=True)
    spread = jnp.mean((values - centre) * (values - centre), axis=-1, keepdims=True)
    return (values - centre) * lax.rsqrt(spread + 1e-05)


def predict(weight, velocity, scales):
    return (
        weight.astype(jnp.float32)[None]
        + scales[:, None, None] * velocity.astype(jnp.float32)[None]
    ).astype(jnp.bfloat16)


def plane_mats(shape):
    rows = int(np.prod(shape))
    coords = np.stack(np.unravel_index(np.arange(rows), shape), axis=1)
    strides = [int(np.prod(shape[a + 1:])) for a in range(3)]
    counts = [rows // shape[a] for a in range(3)]
    offsets = [sum(counts[:a]) for a in range(3)]
    planes = sum(counts)
    up = np.zeros((3 * rows, rows), np.float32)
    t_up = np.zeros((3 * rows, planes), np.float32)
    bots = np.zeros((planes, rows), np.float32)
    tops = np.zeros((planes, rows), np.float32)
    total = np.zeros((rows, 3 * rows), np.float32)
    t_down = np.zeros((rows, planes), np.float32)
    for a in range(3):
        length = shape[a]
        index = np.zeros(rows, np.int64)
        for edge in range(length):
            picked = np.nonzero(coords[:, a] == edge)[0]
            index[picked] = np.arange(picked.size)
        for r in range(rows):
            c = coords[r, a]
            p = offsets[a] + index[r]
            total[r, a * rows + r] = 1
            if c == 0:
                bots[p, r] = 1
                t_down[r, p] = 1
            else:
                total[r, a * rows + r - strides[a]] = 1
            if c == length - 1:
                tops[p, r] = 1
                t_up[a * rows + r, p] = 1
            else:
                up[a * rows + r, r + strides[a]] = 1
    return tuple(jnp.asarray(m, jnp.bfloat16) for m in (up, t_up, bots, tops, total, t_down))


def dot(a, b):
    return jnp.dot(a, b, preferred_element_type=jnp.float32)


def layer_kernel(*refs):
    idx = refs[0]
    (h_ref, e_ref, g0, g1, g2, a0, a1, a2, b0, b1, b2, temb_ref, mine_ref, other_ref, scale_ref,
     omask_ref) = refs[1:17]
    up, t_up, bots, tops, total_m, t_down = (m[...] for m in refs[17:23])
    outs = refs[23:]
    h_out, e_out = outs[0], outs[1]
    g_out = outs[2:5]
    bot_out = outs[5:8]
    top_out = outs[8:11]
    ghosts = (g0, g1, g2)
    aboves = (a0, a1, a2)
    belows = (b0, b1, b2)
    width = h_ref.shape[-1]
    rows = h_ref.shape[1]
    counts = [g.shape[1] for g in ghosts]
    offsets = [sum(counts[:a]) for a in range(3)]
    planes = sum(counts)
    sizes = (3 * width, width, 2 * width, width)
    starts = [sum(sizes[:i]) for i in range(4)]
    core_zero = idx[1] == 0
    mine = mine_ref[0]
    other = other_ref[0]
    w_all = jnp.where(core_zero, mine, other).astype(jnp.float32)
    v_all = jnp.where(core_zero, other, mine).astype(jnp.float32)
    plane_row = lax.broadcasted_iota(jnp.int32, (planes, width), 0)
    lower = jnp.where(
        plane_row < offsets[1], idx[2], jnp.where(plane_row < offsets[2], idx[3], idx[4])
    )
    omask = omask_ref[...]
    for b in range(h_ref.shape[0]):
        scale = scale_ref[b:b + 1, :]
        pred = (w_all + scale * v_all).astype(jnp.bfloat16)
        w1, w2, n1, n2 = (pred[starts[i]:starts[i] + sizes[i]] for i in range(4))
        h = h_ref[b]
        w1e, w1s, w1d = w1[:width], w1[width:2 * width], w1[2 * width:]
        above = jnp.concatenate([aboves[d][b] for d in range(3)], axis=0)
        below = jnp.concatenate([belows[d][b] for d in range(3)], axis=0)
        g = jnp.concatenate([ghosts[d][b] for d in range(3)], axis=0)
        e = jnp.concatenate([e_ref[d, b] for d in range(3)], axis=0)
        h_src = dot(h, w1s)
        nxt = (dot(up, h) + dot(t_up, above)).astype(jnp.bfloat16)
        pre = dot(e, w1e) + jnp.concatenate([h_src] * 3, axis=0) + dot(nxt, w1d)
        hid = jnp.maximum(pre, 0.0).astype(jnp.bfloat16)
        fresh = e.astype(jnp.float32) + layer_norm(dot(hid, w2))
        fresh = jnp.where(omask > 0.5, fresh, 0.0).astype(jnp.bfloat16)
        bottom = dot(bots, h).astype(jnp.bfloat16)
        pre_g = dot(g, w1e) + dot(below, w1s) + dot(bottom, w1d)
        hid_g = jnp.maximum(pre_g, 0.0).astype(jnp.bfloat16)
        ghost = g.astype(jnp.float32) + layer_norm(dot(hid_g, w2))
        ghost = jnp.where(lower > 0, ghost, 0.0).astype(jnp.bfloat16)
        total = dot(total_m, fresh) + dot(t_down, ghost)
        for d in range(3):
            e_out[d, b] = fresh[d * rows:(d + 1) * rows]
            g_out[d][b] = ghost[offsets[d]:offsets[d] + counts[d]]
        pre = dot(h, n1[:width]) + dot(total.astype(jnp.bfloat16), n1[width:]) + temb_ref[...]
        hid = jnp.maximum(pre, 0.0).astype(jnp.bfloat16)
        h_new = (h.astype(jnp.float32) + layer_norm(dot(hid, n2))).astype(jnp.bfloat16)
        h_out[b] = h_new
        bot_new = dot(bots, h_new).astype(jnp.bfloat16)
        top_new = dot(tops, h_new).astype(jnp.bfloat16)
        for d in range(3):
            bot_out[d][b] = bot_new[offsets[d]:offsets[d] + counts[d]]
            top_out[d][b] = top_new[offsets[d]:offsets[d] + counts[d]]


def whole(shape):
    return pl.BlockSpec(shape, lambda i, idx: (0,) * len(shape))


def run_layer(idx, h, e, ghosts, aboves, belows, temb, mine_all, other_all, scales, omask, mats):
    batch, rows, width = h.shape
    counts = [g.shape[1] for g in ghosts]
    out_shape = (
        [jax.ShapeDtypeStruct(h.shape, h.dtype), jax.ShapeDtypeStruct(e.shape, e.dtype)]
        + [jax.ShapeDtypeStruct(g.shape, g.dtype) for g in ghosts]
        + [jax.ShapeDtypeStruct((batch, c, width), h.dtype) for c in counts] * 2
    )
    flat_mats = list(mats)
    layer_block = (1,) + mine_all.shape[1:]
    operands = [h, e, *ghosts, *aboves, *belows, temb]
    in_specs = [whole(x.shape) for x in operands]
    in_specs += [pl.BlockSpec(layer_block, lambda i, idx: (idx[0], 0, 0))] * 2
    tail = [scales, omask, *flat_mats]
    in_specs += [whole(x.shape) for x in tail]
    grid_spec = pltpu.PrefetchScalarGridSpec(
        num_scalar_prefetch=1,
        grid=(1,),
        in_specs=in_specs,
        out_specs=[whole(o.shape) for o in out_shape],
    )
    res = pl.pallas_call(
        layer_kernel,
        out_shape=out_shape,
        grid_spec=grid_spec,
        input_output_aliases={1: 0, 2: 1, 3: 2, 4: 3, 5: 4},
    )(idx, *operands, mine_all, other_all, *tail)
    return res[0], res[1], tuple(res[2:5]), tuple(res[5:8]), tuple(res[8:11])


def local(
    nodes_in,
    edges_in,
    codes,
    type_table,
    order,
    edge_w1,
    edge_w2,
    node_w1,
    node_w2,
    edge_v1,
    edge_v2,
    node_v1,
    node_v2,
):
    section_count = lax.axis_size("section")
    section_id = lax.axis_index("section")
    count_z = lax.axis_size("space") // 16
    space_id = lax.axis_index("space")
    coords = (space_id // (4 * count_z), space_id // count_z % 4, space_id % count_z)
    counts = (4, 4, count_z)
    strides = (4 * count_z, count_z, 1)
    width = nodes_in.shape[-1]
    local_count = nodes_in.shape[0]
    rows = nodes_in.shape[1]
    batches = local_count * section_count
    type_ids = lax.broadcasted_iota(jnp.int32, (codes.shape[0], type_table.shape[0]), 1)
    one_hot = (codes[:, None] == type_ids).astype(jnp.float32)
    type_embed = jnp.sum(one_hot[:, :, None] * type_table[None, :, :], axis=1)
    divisor = jnp.float32(batches + 2 * section_count)

    mine = section_id * local_count + jnp.arange(local_count, dtype=jnp.int32)
    slots = jnp.arange(batches, dtype=jnp.int32)
    position = jnp.sum(
        jnp.where(order[None, :] == mine[:, None], slots[None, :], 0), axis=1
    )

    core = space_id % 2
    sizes = [w.shape[1] for w in (edge_w1, edge_w2, node_w1, node_w2)]
    halves = (
        jnp.concatenate([edge_w1[0], edge_w2[0], node_w1[0], node_w2[0]], axis=0),
        jnp.concatenate([edge_v1[0], edge_v2[0], node_v1[0], node_v2[0]], axis=0),
    )
    own_half = jnp.where(core == 0, halves[0], halves[1])
    space_count = lax.axis_size("space")
    ring = 4
    ring_stride = space_count // ring
    ring_pos = coords[0]
    chunk = own_half.shape[0] // ring
    my_part = lax.dynamic_slice_in_dim(own_half, ring_pos * chunk, chunk, axis=0)
    layers = jnp.zeros((section_count,) + my_part.shape, my_part.dtype)
    layers = lax.dynamic_update_slice_in_dim(layers, my_part[None], section_id, axis=0)
    for k in range(1, section_count):
        shift = [(i, (i + k) % section_count) for i in range(section_count)]
        layers = lax.dynamic_update_slice_in_dim(
            layers,
            lax.ppermute(my_part, "section", shift)[None],
            (section_id - k) % section_count,
            axis=0,
        )
    got = [layers]
    for k in range(1, ring):
        shift = [(i, (i + k * ring_stride) % space_count) for i in range(space_count)]
        got.append(lax.ppermute(got[0], "space", shift))
    own_all = jnp.zeros((section_count, ring * chunk, own_half.shape[1]), own_half.dtype)
    for k in range(ring):
        own_all = lax.dynamic_update_slice_in_dim(
            own_all, got[k], (ring_pos - k) % ring * chunk, axis=1
        )
    swap = [(i, i ^ 1) for i in range(space_count)]
    other_all = lax.ppermute(own_all, "space", swap)
    starts = [sum(sizes[:i]) for i in range(4)]

    shape = (BX, BY, BZ)
    mats = plane_mats(shape)
    grid_pos = np.stack(np.unravel_index(np.arange(rows), shape), axis=1)
    omask = jnp.stack(
        [
            jnp.broadcast_to(
                (coords[a] * shape[a] + grid_pos[:, a] < shape[a] * counts[a] - 1)[:, None],
                (rows, width),
            ).astype(jnp.float32)
            for a in range(3)
        ]
    ).reshape(3 * rows, width)
    h0 = nodes_in
    e0 = jnp.transpose(edges_in, (1, 0, 2, 3))
    plane_counts = [rows // shape[a] for a in range(3)]
    plane_offsets = [sum(plane_counts[:a]) for a in range(3)]

    def split_planes(stacked):
        return tuple(
            stacked[:, plane_offsets[a]:plane_offsets[a] + plane_counts[a]] for a in range(3)
        )

    bot0 = split_planes(jnp.einsum("pr,brw->bpw", mats[2], h0).astype(jnp.bfloat16))
    top0 = split_planes(jnp.einsum("pr,brw->bpw", mats[3], h0).astype(jnp.bfloat16))
    ghosts0 = tuple(
        along_line(
            split_planes(jnp.einsum("pr,brw->bpw", mats[3], e0[a]).astype(jnp.bfloat16))[a],
            strides[a],
            strides[a],
            counts[a],
        )
        for a in range(3)
    )

    lower_flags = [(coords[a] > 0).astype(jnp.int32) for a in range(3)]

    def layer_step(layer_id, carry):
        h, e, ghosts, bots, tops = carry
        scales = (position + 2 * section_count - 2 - layer_id).astype(jnp.float32) / divisor
        scales = jnp.broadcast_to(scales[:, None], (local_count, width))
        idx = jnp.stack([layer_id, core] + lower_flags).astype(jnp.int32)
        aboves = tuple(along_line(bots[a], -strides[a], strides[a], counts[a]) for a in range(3))
        belows = tuple(along_line(tops[a], strides[a], strides[a], counts[a]) for a in range(3))
        return run_layer(
            idx, h, e, ghosts, aboves, belows, type_embed, own_all, other_all, scales, omask, mats
        )

    h, _, _, _, _ = lax.fori_loop(
        0, section_count, layer_step, (h0, e0, ghosts0, bot0, top0)
    )
    return h


def solution(mesh):
    return jax.shard_map(
        local,
        mesh=mesh,
        in_specs=(
            P("section", "space", None),
            P("section", None, "space", None),
            P("space"),
            P(),
            P(),
            P("section", None, None),
            P("section", None, None),
            P("section", None, None),
            P("section", None, None),
            P("section", None, None),
            P("section", None, None),
            P("section", None, None),
            P("section", None, None),
        ),
        out_specs=P("section", "space", None),
        check_vma=False,
    )
```

```python
import jax
import jax.numpy as jnp
from jax import lax
from jax.sharding import PartitionSpec as P
from jax.experimental import pallas as pl
from jax.experimental.pallas import tpu as pltpu
import numpy as np

BX = 8
BY = 4
BZ = 4


def from_behind(shard, axis, by):
    peers = lax.axis_size(axis)
    pairs = [(i, i + by) for i in range(peers) if 0 <= i + by < peers]
    return lax.ppermute(shard, axis, pairs)


def along_line(shard, by, stride, count):
    peers = lax.axis_size("space")
    step = by // stride
    pairs = [
        (i, i + by) for i in range(peers) if 0 <= (i // stride) % count + step < count
    ]
    return lax.ppermute(shard, "space", pairs)


def layer_norm(values):
    centre = jnp.mean(values, axis=-1, keepdims=True)
    spread = jnp.mean((values - centre) * (values - centre), axis=-1, keepdims=True)
    return (values - centre) * lax.rsqrt(spread + 1e-05)


def predict(weight, velocity, scales):
    return (
        weight.astype(jnp.float32)[None]
        + scales[:, None, None] * velocity.astype(jnp.float32)[None]
    ).astype(jnp.bfloat16)


def plane_mats(shape):
    rows = int(np.prod(shape))
    coords = np.stack(np.unravel_index(np.arange(rows), shape), axis=1)
    strides = [int(np.prod(shape[a + 1:])) for a in range(3)]
    counts = [rows // shape[a] for a in range(3)]
    offsets = [sum(counts[:a]) for a in range(3)]
    planes = sum(counts)
    up = np.zeros((3 * rows, rows), np.float32)
    t_up = np.zeros((3 * rows, planes), np.float32)
    bots = np.zeros((planes, rows), np.float32)
    tops = np.zeros((planes, rows), np.float32)
    total = np.zeros((rows, 3 * rows), np.float32)
    t_down = np.zeros((rows, planes), np.float32)
    for a in range(3):
        length = shape[a]
        index = np.zeros(rows, np.int64)
        for edge in range(length):
            picked = np.nonzero(coords[:, a] == edge)[0]
            index[picked] = np.arange(picked.size)
        for r in range(rows):
            c = coords[r, a]
            p = offsets[a] + index[r]
            total[r, a * rows + r] = 1
            if c == 0:
                bots[p, r] = 1
                t_down[r, p] = 1
            else:
                total[r, a * rows + r - strides[a]] = 1
            if c == length - 1:
                tops[p, r] = 1
                t_up[a * rows + r, p] = 1
            else:
                up[a * rows + r, r + strides[a]] = 1
    return tuple(jnp.asarray(m, jnp.bfloat16) for m in (up, t_up, bots, tops, total, t_down))


def dot(a, b):
    return jnp.dot(a, b, preferred_element_type=jnp.float32)


def layer_kernel(*refs):
    idx = refs[0]
    (h_ref, e_ref, g0, g1, g2, a0, a1, a2, b0, b1, b2, temb_ref, mine_ref, other_ref, scale_ref,
     omask_ref) = refs[1:17]
    up, t_up, bots, tops, total_m, t_down = (m[...] for m in refs[17:23])
    outs = refs[23:]
    h_out, e_out = outs[0], outs[1]
    g_out = outs[2:5]
    bot_out = outs[5:8]
    top_out = outs[8:11]
    ghosts = (g0, g1, g2)
    aboves = (a0, a1, a2)
    belows = (b0, b1, b2)
    width = h_ref.shape[-1]
    rows = h_ref.shape[1]
    counts = [g.shape[1] for g in ghosts]
    offsets = [sum(counts[:a]) for a in range(3)]
    planes = sum(counts)
    sizes = (3 * width, width, 2 * width, width)
    starts = [sum(sizes[:i]) for i in range(4)]
    core_zero = idx[1] == 0
    mine = mine_ref[0]
    other = other_ref[0]
    w_all = jnp.where(core_zero, mine, other).astype(jnp.float32)
    v_all = jnp.where(core_zero, other, mine).astype(jnp.float32)
    plane_row = lax.broadcasted_iota(jnp.int32, (planes, width), 0)
    lower = jnp.where(
        plane_row < offsets[1], idx[2], jnp.where(plane_row < offsets[2], idx[3], idx[4])
    )
    omask = omask_ref[...]
    for b in range(h_ref.shape[0]):
        scale = scale_ref[b:b + 1, :]
        pred = (w_all + scale * v_all).astype(jnp.bfloat16)
        w1, w2, n1, n2 = (pred[starts[i]:starts[i] + sizes[i]] for i in range(4))
        h = h_ref[b]
        w1e, w1s, w1d = w1[:width], w1[width:2 * width], w1[2 * width:]
        above = jnp.concatenate([aboves[d][b] for d in range(3)], axis=0)
        below = jnp.concatenate([belows[d][b] for d in range(3)], axis=0)
        g = jnp.concatenate([ghosts[d][b] for d in range(3)], axis=0)
        e = jnp.concatenate([e_ref[d, b] for d in range(3)], axis=0)
        h_src = dot(h, w1s)
        nxt = (dot(up, h) + dot(t_up, above)).astype(jnp.bfloat16)
        pre = dot(e, w1e) + jnp.concatenate([h_src] * 3, axis=0) + dot(nxt, w1d)
        hid = jnp.maximum(pre, 0.0).astype(jnp.bfloat16)
        fresh = e.astype(jnp.float32) + layer_norm(dot(hid, w2))
        fresh = jnp.where(omask > 0.5, fresh, 0.0).astype(jnp.bfloat16)
        bottom = dot(bots, h).astype(jnp.bfloat16)
        pre_g = dot(g, w1e) + dot(below, w1s) + dot(bottom, w1d)
        hid_g = jnp.maximum(pre_g, 0.0).astype(jnp.bfloat16)
        ghost = g.astype(jnp.float32) + layer_norm(dot(hid_g, w2))
        ghost = jnp.where(lower > 0, ghost, 0.0).astype(jnp.bfloat16)
        total = dot(total_m, fresh) + dot(t_down, ghost)
        for d in range(3):
            e_out[d, b] = fresh[d * rows:(d + 1) * rows]
            g_out[d][b] = ghost[offsets[d]:offsets[d] + counts[d]]
        pre = dot(h, n1[:width]) + dot(total.astype(jnp.bfloat16), n1[width:]) + temb_ref[...]
        hid = jnp.maximum(pre, 0.0).astype(jnp.bfloat16)
        h_new = (h.astype(jnp.float32) + layer_norm(dot(hid, n2))).astype(jnp.bfloat16)
        h_out[b] = h_new
        bot_new = dot(bots, h_new).astype(jnp.bfloat16)
        top_new = dot(tops, h_new).astype(jnp.bfloat16)
        for d in range(3):
            bot_out[d][b] = bot_new[offsets[d]:offsets[d] + counts[d]]
            top_out[d][b] = top_new[offsets[d]:offsets[d] + counts[d]]


def whole(shape):
    return pl.BlockSpec(shape, lambda i, idx: (0,) * len(shape))


def run_layer(idx, h, e, ghosts, aboves, belows, temb, mine_all, other_all, scales, omask, mats):
    batch, rows, width = h.shape
    counts = [g.shape[1] for g in ghosts]
    out_shape = (
        [jax.ShapeDtypeStruct(h.shape, h.dtype), jax.ShapeDtypeStruct(e.shape, e.dtype)]
        + [jax.ShapeDtypeStruct(g.shape, g.dtype) for g in ghosts]
        + [jax.ShapeDtypeStruct((batch, c, width), h.dtype) for c in counts] * 2
    )
    flat_mats = list(mats)
    layer_block = (1,) + mine_all.shape[1:]
    operands = [h, e, *ghosts, *aboves, *belows, temb]
    in_specs = [whole(x.shape) for x in operands]
    in_specs += [pl.BlockSpec(layer_block, lambda i, idx: (idx[0], 0, 0))] * 2
    tail = [scales, omask, *flat_mats]
    in_specs += [whole(x.shape) for x in tail]
    grid_spec = pltpu.PrefetchScalarGridSpec(
        num_scalar_prefetch=1,
        grid=(1,),
        in_specs=in_specs,
        out_specs=[whole(o.shape) for o in out_shape],
    )
    res = pl.pallas_call(
        layer_kernel,
        out_shape=out_shape,
        grid_spec=grid_spec,
        input_output_aliases={1: 0, 2: 1, 3: 2, 4: 3, 5: 4},
    )(idx, *operands, mine_all, other_all, *tail)
    return res[0], res[1], tuple(res[2:5]), tuple(res[5:8]), tuple(res[8:11])


def local(
    nodes_in,
    edges_in,
    codes,
    type_table,
    order,
    edge_w1,
    edge_w2,
    node_w1,
    node_w2,
    edge_v1,
    edge_v2,
    node_v1,
    node_v2,
):
    section_count = lax.axis_size("section")
    section_id = lax.axis_index("section")
    count_z = lax.axis_size("space") // 16
    space_id = lax.axis_index("space")
    coords = (space_id // (4 * count_z), space_id // count_z % 4, space_id % count_z)
    counts = (4, 4, count_z)
    strides = (4 * count_z, count_z, 1)
    width = nodes_in.shape[-1]
    local_count = nodes_in.shape[0]
    rows = nodes_in.shape[1]
    batches = local_count * section_count
    type_ids = lax.broadcasted_iota(jnp.int32, (codes.shape[0], type_table.shape[0]), 1)
    one_hot = (codes[:, None] == type_ids).astype(jnp.float32)
    type_embed = jnp.sum(one_hot[:, :, None] * type_table[None, :, :], axis=1)
    divisor = jnp.float32(batches + 2 * section_count)

    mine = section_id * local_count + jnp.arange(local_count, dtype=jnp.int32)
    slots = jnp.arange(batches, dtype=jnp.int32)
    position = jnp.sum(
        jnp.where(order[None, :] == mine[:, None], slots[None, :], 0), axis=1
    )

    core = space_id % 2
    sizes = [w.shape[1] for w in (edge_w1, edge_w2, node_w1, node_w2)]
    halves = (
        jnp.concatenate([edge_w1[0], edge_w2[0], node_w1[0], node_w2[0]], axis=0),
        jnp.concatenate([edge_v1[0], edge_v2[0], node_v1[0], node_v2[0]], axis=0),
    )
    own_half = jnp.where(core == 0, halves[0], halves[1])
    space_count = lax.axis_size("space")
    ring = 4
    ring_stride = space_count // ring
    ring_pos = space_id // ring_stride
    pair_bit = space_id // 2 % 2
    group = 2 * ring
    chunk = own_half.shape[0] // group
    part_of = lambda ring_at, bit: ring_at * 2 + bit
    my_part = lax.dynamic_slice_in_dim(
        own_half, part_of(ring_pos, pair_bit) * chunk, chunk, axis=0
    )
    layers = jnp.zeros((section_count,) + my_part.shape, my_part.dtype)
    layers = lax.dynamic_update_slice_in_dim(layers, my_part[None], section_id, axis=0)
    for k in range(1, section_count):
        shift = [(i, (i + k) % section_count) for i in range(section_count)]
        layers = lax.dynamic_update_slice_in_dim(
            layers,
            lax.ppermute(my_part, "section", shift)[None],
            (section_id - k) % section_count,
            axis=0,
        )
    own_all = jnp.zeros((section_count, group * chunk, own_half.shape[1]), own_half.dtype)
    for dx in range(ring):
        for dz in range(2):
            if dx == 0 and dz == 0:
                got = layers
            else:
                moves = [
                    (i, (i // ring_stride + dx) % ring * ring_stride + ((i % ring_stride) ^ (2 * dz)))
                    for i in range(space_count)
                ]
                got = lax.ppermute(layers, "space", moves)
            source = part_of((ring_pos - dx) % ring, pair_bit ^ dz)
            own_all = lax.dynamic_update_slice_in_dim(own_all, got, source * chunk, axis=1)
    swap = [(i, i ^ 1) for i in range(space_count)]
    other_all = lax.ppermute(own_all, "space", swap)
    starts = [sum(sizes[:i]) for i in range(4)]

    shape = (BX, BY, BZ)
    mats = plane_mats(shape)
    grid_pos = np.stack(np.unravel_index(np.arange(rows), shape), axis=1)
    omask = jnp.stack(
        [
            jnp.broadcast_to(
                (coords[a] * shape[a] + grid_pos[:, a] < shape[a] * counts[a] - 1)[:, None],
                (rows, width),
            ).astype(jnp.float32)
            for a in range(3)
        ]
    ).reshape(3 * rows, width)
    h0 = nodes_in
    e0 = jnp.transpose(edges_in, (1, 0, 2, 3))
    plane_counts = [rows // shape[a] for a in range(3)]
    plane_offsets = [sum(plane_counts[:a]) for a in range(3)]

    def split_planes(stacked):
        return tuple(
            stacked[:, plane_offsets[a]:plane_offsets[a] + plane_counts[a]] for a in range(3)
        )

    bot0 = split_planes(jnp.einsum("pr,brw->bpw", mats[2], h0).astype(jnp.bfloat16))
    top0 = split_planes(jnp.einsum("pr,brw->bpw", mats[3], h0).astype(jnp.bfloat16))
    ghosts0 = tuple(
        along_line(
            split_planes(jnp.einsum("pr,brw->bpw", mats[3], e0[a]).astype(jnp.bfloat16))[a],
            strides[a],
            strides[a],
            counts[a],
        )
        for a in range(3)
    )

    lower_flags = [(coords[a] > 0).astype(jnp.int32) for a in range(3)]

    def layer_step(layer_id, carry):
        h, e, ghosts, bots, tops = carry
        scales = (position + 2 * section_count - 2 - layer_id).astype(jnp.float32) / divisor
        scales = jnp.broadcast_to(scales[:, None], (local_count, width))
        idx = jnp.stack([layer_id, core] + lower_flags).astype(jnp.int32)
        aboves = tuple(along_line(bots[a], -strides[a], strides[a], counts[a]) for a in range(3))
        belows = tuple(along_line(tops[a], strides[a], strides[a], counts[a]) for a in range(3))
        return run_layer(
            idx, h, e, ghosts, aboves, belows, type_embed, own_all, other_all, scales, omask, mats
        )

    h, _, _, _, _ = lax.fori_loop(
        0, section_count, layer_step, (h0, e0, ghosts0, bot0, top0)
    )
    return h


def solution(mesh):
    return jax.shard_map(
        local,
        mesh=mesh,
        in_specs=(
            P("section", "space", None),
            P("section", None, "space", None),
            P("space"),
            P(),
            P(),
            P("section", None, None),
            P("section", None, None),
            P("section", None, None),
            P("section", None, None),
            P("section", None, None),
            P("section", None, None),
            P("section", None, None),
            P("section", None, None),
        ),
        out_specs=P("section", "space", None),
        check_vma=False,
    )
```

```python
import jax
import jax.numpy as jnp
from jax import lax
from jax.sharding import PartitionSpec as P
from jax.experimental import pallas as pl
from jax.experimental.pallas import tpu as pltpu
import numpy as np


BX = 8
BY = 4
BZ = 4


def from_behind(shard, axis, by):
    peers = lax.axis_size(axis)
    pairs = [(i, i + by) for i in range(peers) if 0 <= i + by < peers]
    return lax.ppermute(shard, axis, pairs)


def along_line(shard, by, stride, count):
    peers = lax.axis_size("space")
    step = by // stride
    pairs = [
        (i, i + by) for i in range(peers) if 0 <= (i // stride) % count + step < count
    ]
    return lax.ppermute(shard, "space", pairs)


def layer_norm(values):
    centre = jnp.mean(values, axis=-1, keepdims=True)
    spread = jnp.mean((values - centre) * (values - centre), axis=-1, keepdims=True)
    return (values - centre) * lax.rsqrt(spread + 1e-05)


def predict(weight, velocity, scales):
    return (
        weight.astype(jnp.float32)[None]
        + scales[:, None, None] * velocity.astype(jnp.float32)[None]
    ).astype(jnp.bfloat16)


def plane_mats(shape):
    rows = int(np.prod(shape))
    coords = np.stack(np.unravel_index(np.arange(rows), shape), axis=1)
    strides = [int(np.prod(shape[a + 1:])) for a in range(3)]
    counts = [rows // shape[a] for a in range(3)]
    offsets = [sum(counts[:a]) for a in range(3)]
    planes = sum(counts)
    up = np.zeros((3 * rows, rows), np.float32)
    t_up = np.zeros((3 * rows, planes), np.float32)
    bots = np.zeros((planes, rows), np.float32)
    tops = np.zeros((planes, rows), np.float32)
    total = np.zeros((rows, 3 * rows), np.float32)
    t_down = np.zeros((rows, planes), np.float32)
    for a in range(3):
        length = shape[a]
        index = np.zeros(rows, np.int64)
        for edge in range(length):
            picked = np.nonzero(coords[:, a] == edge)[0]
            index[picked] = np.arange(picked.size)
        for r in range(rows):
            c = coords[r, a]
            p = offsets[a] + index[r]
            total[r, a * rows + r] = 1
            if c == 0:
                bots[p, r] = 1
                t_down[r, p] = 1
            else:
                total[r, a * rows + r - strides[a]] = 1
            if c == length - 1:
                tops[p, r] = 1
                t_up[a * rows + r, p] = 1
            else:
                up[a * rows + r, r + strides[a]] = 1
    return tuple(jnp.asarray(m, jnp.bfloat16) for m in (up, t_up, bots, tops, total, t_down))


def dot(a, b):
    return jnp.dot(a, b, preferred_element_type=jnp.float32)


def layer_kernel(*refs):
    idx = refs[1]
    (h_ref, e_ref, g0, g1, g2, a0, a1, a2, b0, b1, b2, temb_ref, mine_ref, other_ref, scale_ref,
     omask_ref) = refs[2:18]
    up, t_up, bots, tops, total_m, t_down = (m[...] for m in refs[18:24])
    outs = refs[24:]
    h_out, e_out = outs[0], outs[1]
    g_out = outs[2:5]
    bot_out = outs[5:8]
    top_out = outs[8:11]
    ghosts = (g0, g1, g2)
    aboves = (a0, a1, a2)
    belows = (b0, b1, b2)
    width = h_ref.shape[-1]
    rows = h_ref.shape[1]
    counts = [g.shape[1] for g in ghosts]
    offsets = [sum(counts[:a]) for a in range(3)]
    planes = sum(counts)
    sizes = (3 * width, width, 2 * width, width)
    starts = [sum(sizes[:i]) for i in range(4)]
    core_zero = idx[0] == 0
    mine = mine_ref[0]
    other = other_ref[0]
    w_all = jnp.where(core_zero, mine, other).astype(jnp.float32)
    v_all = jnp.where(core_zero, other, mine).astype(jnp.float32)
    plane_row = lax.broadcasted_iota(jnp.int32, (planes, width), 0)
    lower = jnp.where(
        plane_row < offsets[1], idx[1], jnp.where(plane_row < offsets[2], idx[2], idx[3])
    )
    omask = omask_ref[...]
    for b in range(h_ref.shape[0]):
        scale = scale_ref[0, b:b + 1, :]
        pred = (w_all + scale * v_all).astype(jnp.bfloat16)
        w1, w2, n1, n2 = (pred[starts[i]:starts[i] + sizes[i]] for i in range(4))
        h = h_ref[b]
        w1e, w1s, w1d = w1[:width], w1[width:2 * width], w1[2 * width:]
        above = jnp.concatenate([aboves[d][b] for d in range(3)], axis=0)
        below = jnp.concatenate([belows[d][b] for d in range(3)], axis=0)
        g = jnp.concatenate([ghosts[d][b] for d in range(3)], axis=0)
        e = jnp.concatenate([e_ref[d, b] for d in range(3)], axis=0)
        h_src = dot(h, w1s)
        nxt = (dot(up, h) + dot(t_up, above)).astype(jnp.bfloat16)
        pre = dot(e, w1e) + jnp.concatenate([h_src] * 3, axis=0) + dot(nxt, w1d)
        hid = jnp.maximum(pre, 0.0).astype(jnp.bfloat16)
        fresh = e.astype(jnp.float32) + layer_norm(dot(hid, w2))
        fresh = jnp.where(omask > 0.5, fresh, 0.0).astype(jnp.bfloat16)
        bottom = dot(bots, h).astype(jnp.bfloat16)
        pre_g = dot(g, w1e) + dot(below, w1s) + dot(bottom, w1d)
        hid_g = jnp.maximum(pre_g, 0.0).astype(jnp.bfloat16)
        ghost = g.astype(jnp.float32) + layer_norm(dot(hid_g, w2))
        ghost = jnp.where(lower > 0, ghost, 0.0).astype(jnp.bfloat16)
        total = dot(total_m, fresh) + dot(t_down, ghost)
        for d in range(3):
            e_out[d, b] = fresh[d * rows:(d + 1) * rows]
            g_out[d][b] = ghost[offsets[d]:offsets[d] + counts[d]]
        pre = dot(h, n1[:width]) + dot(total.astype(jnp.bfloat16), n1[width:]) + temb_ref[...]
        hid = jnp.maximum(pre, 0.0).astype(jnp.bfloat16)
        h_new = (h.astype(jnp.float32) + layer_norm(dot(hid, n2))).astype(jnp.bfloat16)
        h_out[b] = h_new
        bot_new = dot(bots, h_new).astype(jnp.bfloat16)
        top_new = dot(tops, h_new).astype(jnp.bfloat16)
        for d in range(3):
            bot_out[d][b] = bot_new[offsets[d]:offsets[d] + counts[d]]
            top_out[d][b] = top_new[offsets[d]:offsets[d] + counts[d]]


def whole(shape):
    return pl.BlockSpec(shape, lambda i, layer, flags: (0,) * len(shape))


def run_layer(layer, flags, h, e, ghosts, aboves, belows, temb, mine_all, other_all, scales, omask, mats):
    batch, rows, width = h.shape
    counts = [g.shape[1] for g in ghosts]
    out_shape = (
        [jax.ShapeDtypeStruct(h.shape, h.dtype), jax.ShapeDtypeStruct(e.shape, e.dtype)]
        + [jax.ShapeDtypeStruct(g.shape, g.dtype) for g in ghosts]
        + [jax.ShapeDtypeStruct((batch, c, width), h.dtype) for c in counts] * 2
    )
    flat_mats = list(mats)
    layer_block = (1,) + mine_all.shape[1:]
    operands = [h, e, *ghosts, *aboves, *belows, temb]
    in_specs = [whole(x.shape) for x in operands]
    in_specs += [pl.BlockSpec(layer_block, lambda i, layer, flags: (layer[0], 0, 0))] * 2
    in_specs += [pl.BlockSpec((1,) + scales.shape[1:], lambda i, layer, flags: (layer[0], 0, 0))]
    tail = [omask, *flat_mats]
    in_specs += [whole(x.shape) for x in tail]
    grid_spec = pltpu.PrefetchScalarGridSpec(
        num_scalar_prefetch=2,
        grid=(1,),
        in_specs=in_specs,
        out_specs=[whole(o.shape) for o in out_shape],
    )
    res = pl.pallas_call(
        layer_kernel,
        out_shape=out_shape,
        grid_spec=grid_spec,
        input_output_aliases={2: 0, 3: 1, 4: 2, 5: 3, 6: 4},
    )(layer, flags, *operands, mine_all, other_all, scales, *tail)
    return res[0], res[1], tuple(res[2:5]), tuple(res[5:8]), tuple(res[8:11])


def local(
    nodes_in,
    edges_in,
    codes,
    type_table,
    order,
    edge_w1,
    edge_w2,
    node_w1,
    node_w2,
    edge_v1,
    edge_v2,
    node_v1,
    node_v2,
):
    section_count = lax.axis_size("section")
    section_id = lax.axis_index("section")
    count_z = lax.axis_size("space") // 16
    space_id = lax.axis_index("space")
    coords = (space_id // (4 * count_z), space_id // count_z % 4, space_id % count_z)
    counts = (4, 4, count_z)
    strides = (4 * count_z, count_z, 1)
    width = nodes_in.shape[-1]
    local_count = nodes_in.shape[0]
    rows = nodes_in.shape[1]
    batches = local_count * section_count
    type_ids = lax.broadcasted_iota(jnp.int32, (codes.shape[0], type_table.shape[0]), 1)
    one_hot = (codes[:, None] == type_ids).astype(jnp.float32)
    type_embed = jnp.sum(one_hot[:, :, None] * type_table[None, :, :], axis=1)
    divisor = jnp.float32(batches + 2 * section_count)

    mine = section_id * local_count + jnp.arange(local_count, dtype=jnp.int32)
    slots = jnp.arange(batches, dtype=jnp.int32)
    position = jnp.sum(
        jnp.where(order[None, :] == mine[:, None], slots[None, :], 0), axis=1
    )

    core = space_id % 2
    sizes = [w.shape[1] for w in (edge_w1, edge_w2, node_w1, node_w2)]
    halves = (
        jnp.concatenate([edge_w1[0], edge_w2[0], node_w1[0], node_w2[0]], axis=0),
        jnp.concatenate([edge_v1[0], edge_v2[0], node_v1[0], node_v2[0]], axis=0),
    )
    own_half = jnp.where(core == 0, halves[0], halves[1])
    space_count = lax.axis_size("space")
    ring = 4
    ring_stride = space_count // ring
    ring_pos = space_id // ring_stride
    pair_bit = space_id // 2 % 2
    group = 2 * ring
    chunk = own_half.shape[0] // group
    part_of = lambda ring_at, bit: ring_at * 2 + bit
    my_part = lax.dynamic_slice_in_dim(
        own_half, part_of(ring_pos, pair_bit) * chunk, chunk, axis=0
    )
    layers = jnp.zeros((section_count,) + my_part.shape, my_part.dtype)
    layers = lax.dynamic_update_slice_in_dim(layers, my_part[None], section_id, axis=0)
    for k in range(1, section_count):
        shift = [(i, (i + k) % section_count) for i in range(section_count)]
        layers = lax.dynamic_update_slice_in_dim(
            layers,
            lax.ppermute(my_part, "section", shift)[None],
            (section_id - k) % section_count,
            axis=0,
        )
    own_all = jnp.zeros((section_count, group * chunk, own_half.shape[1]), own_half.dtype)
    for dx in range(ring):
        for dz in range(2):
            if dx == 0 and dz == 0:
                got = layers
            else:
                moves = [
                    (i, (i // ring_stride + dx) % ring * ring_stride + ((i % ring_stride) ^ (2 * dz)))
                    for i in range(space_count)
                ]
                got = lax.ppermute(layers, "space", moves)
            source = part_of((ring_pos - dx) % ring, pair_bit ^ dz)
            own_all = lax.dynamic_update_slice_in_dim(own_all, got, source * chunk, axis=1)
    swap = [(i, i ^ 1) for i in range(space_count)]
    other_all = lax.ppermute(own_all, "space", swap)
    starts = [sum(sizes[:i]) for i in range(4)]

    shape = (BX, BY, BZ)
    mats = plane_mats(shape)
    grid_pos = np.stack(np.unravel_index(np.arange(rows), shape), axis=1)
    omask = jnp.stack(
        [
            jnp.broadcast_to(
                (coords[a] * shape[a] + grid_pos[:, a] < shape[a] * counts[a] - 1)[:, None],
                (rows, width),
            ).astype(jnp.float32)
            for a in range(3)
        ]
    ).reshape(3 * rows, width)
    h0 = nodes_in
    e0 = jnp.transpose(edges_in, (1, 0, 2, 3))
    plane_counts = [rows // shape[a] for a in range(3)]
    plane_offsets = [sum(plane_counts[:a]) for a in range(3)]

    def split_planes(stacked):
        return tuple(
            stacked[:, plane_offsets[a]:plane_offsets[a] + plane_counts[a]] for a in range(3)
        )

    bot0 = split_planes(jnp.einsum("pr,brw->bpw", mats[2], h0).astype(jnp.bfloat16))
    top0 = split_planes(jnp.einsum("pr,brw->bpw", mats[3], h0).astype(jnp.bfloat16))
    ghosts0 = tuple(
        along_line(
            split_planes(jnp.einsum("pr,brw->bpw", mats[3], e0[a]).astype(jnp.bfloat16))[a],
            strides[a],
            strides[a],
            counts[a],
        )
        for a in range(3)
    )

    flags = jnp.stack([core] + [(coords[a] > 0).astype(jnp.int32) for a in range(3)]).astype(
        jnp.int32
    )
    layer_ids = jnp.arange(section_count, dtype=jnp.int32)
    all_scales = (
        position[None, :] + 2 * section_count - 2 - layer_ids[:, None]
    ).astype(jnp.float32) / divisor
    all_scales = jnp.broadcast_to(all_scales[:, :, None], (section_count, local_count, width))

    def layer_step(layer_id, carry):
        h, e, ghosts, bots, tops = carry
        layer = jnp.reshape(layer_id, (1,)).astype(jnp.int32)
        aboves = tuple(along_line(bots[a], -strides[a], strides[a], counts[a]) for a in range(3))
        belows = tuple(along_line(tops[a], strides[a], strides[a], counts[a]) for a in range(3))
        return run_layer(
            layer, flags, h, e, ghosts, aboves, belows, type_embed, own_all, other_all,
            all_scales, omask, mats
        )

    h, _, _, _, _ = lax.fori_loop(
        0, section_count, layer_step, (h0, e0, ghosts0, bot0, top0)
    )
    return h


def solution(mesh):
    return jax.shard_map(
        local,
        mesh=mesh,
        in_specs=(
            P("section", "space", None),
            P("section", None, "space", None),
            P("space"),
            P(),
            P(),
            P("section", None, None),
            P("section", None, None),
            P("section", None, None),
            P("section", None, None),
            P("section", None, None),
            P("section", None, None),
            P("section", None, None),
            P("section", None, None),
        ),
        out_specs=P("section", "space", None),
        check_vma=False,
    )
```

```python
import jax
import jax.numpy as jnp
from jax import lax
from jax.sharding import PartitionSpec as P
from jax.experimental import pallas as pl
from jax.experimental.pallas import tpu as pltpu
import numpy as np


BX = 8
BY = 4
BZ = 4


def from_behind(shard, axis, by):
    peers = lax.axis_size(axis)
    pairs = [(i, i + by) for i in range(peers) if 0 <= i + by < peers]
    return lax.ppermute(shard, axis, pairs)


def along_line(shard, by, stride, count):
    peers = lax.axis_size("space")
    step = by // stride
    pairs = [
        (i, i + by) for i in range(peers) if 0 <= (i // stride) % count + step < count
    ]
    return lax.ppermute(shard, "space", pairs)


def layer_norm(values):
    centre = jnp.mean(values, axis=-1, keepdims=True)
    spread = jnp.mean((values - centre) * (values - centre), axis=-1, keepdims=True)
    return (values - centre) * lax.rsqrt(spread + 1e-05)


def predict(weight, velocity, scales):
    return (
        weight.astype(jnp.float32)[None]
        + scales[:, None, None] * velocity.astype(jnp.float32)[None]
    ).astype(jnp.bfloat16)


def plane_mats(shape):
    rows = int(np.prod(shape))
    coords = np.stack(np.unravel_index(np.arange(rows), shape), axis=1)
    strides = [int(np.prod(shape[a + 1:])) for a in range(3)]
    counts = [rows // shape[a] for a in range(3)]
    offsets = [sum(counts[:a]) for a in range(3)]
    planes = sum(counts)
    up = np.zeros((3 * rows, rows), np.float32)
    t_up = np.zeros((3 * rows, planes), np.float32)
    bots = np.zeros((planes, rows), np.float32)
    tops = np.zeros((planes, rows), np.float32)
    total = np.zeros((rows, 3 * rows), np.float32)
    t_down = np.zeros((rows, planes), np.float32)
    for a in range(3):
        length = shape[a]
        index = np.zeros(rows, np.int64)
        for edge in range(length):
            picked = np.nonzero(coords[:, a] == edge)[0]
            index[picked] = np.arange(picked.size)
        for r in range(rows):
            c = coords[r, a]
            p = offsets[a] + index[r]
            total[r, a * rows + r] = 1
            if c == 0:
                bots[p, r] = 1
                t_down[r, p] = 1
            else:
                total[r, a * rows + r - strides[a]] = 1
            if c == length - 1:
                tops[p, r] = 1
                t_up[a * rows + r, p] = 1
            else:
                up[a * rows + r, r + strides[a]] = 1
    return tuple(jnp.asarray(m, jnp.bfloat16) for m in (up, t_up, bots, tops, total, t_down))


def dot(a, b):
    return jnp.dot(a, b, preferred_element_type=jnp.float32)


def layer_kernel(*refs):
    idx = refs[0]
    (h_ref, e_ref, g0, g1, g2, a0, a1, a2, b0, b1, b2, temb_ref, mine_ref, other_ref, scale_ref,
     omask_ref) = refs[1:17]
    up, t_up, bots, tops, total_m, t_down = (m[...] for m in refs[17:23])
    outs = refs[23:]
    h_out, e_out = outs[0], outs[1]
    g_out = outs[2:5]
    bot_out = outs[5:8]
    top_out = outs[8:11]
    ghosts = (g0, g1, g2)
    aboves = (a0, a1, a2)
    belows = (b0, b1, b2)
    width = h_ref.shape[-1]
    rows = h_ref.shape[1]
    counts = [g.shape[1] for g in ghosts]
    offsets = [sum(counts[:a]) for a in range(3)]
    planes = sum(counts)
    sizes = (3 * width, width, 2 * width, width)
    starts = [sum(sizes[:i]) for i in range(4)]
    core_zero = idx[1] == 0
    mine = mine_ref[0]
    other = other_ref[0]
    w_all = jnp.where(core_zero, mine, other).astype(jnp.float32)
    v_all = jnp.where(core_zero, other, mine).astype(jnp.float32)
    plane_row = lax.broadcasted_iota(jnp.int32, (planes, width), 0)
    lower = jnp.where(
        plane_row < offsets[1], idx[2], jnp.where(plane_row < offsets[2], idx[3], idx[4])
    )
    omask = omask_ref[...]
    for b in range(h_ref.shape[0]):
        scale = scale_ref[b:b + 1, :]
        pred = (w_all + scale * v_all).astype(jnp.bfloat16)
        w1, w2, n1, n2 = (pred[starts[i]:starts[i] + sizes[i]] for i in range(4))
        h = h_ref[b]
        w1e, w1s, w1d = w1[:width], w1[width:2 * width], w1[2 * width:]
        above = jnp.concatenate([aboves[d][b] for d in range(3)], axis=0)
        below = jnp.concatenate([belows[d][b] for d in range(3)], axis=0)
        g = jnp.concatenate([ghosts[d][b] for d in range(3)], axis=0)
        e = jnp.concatenate([e_ref[d, b] for d in range(3)], axis=0)
        h_src = dot(h, w1s)
        nxt = (dot(up, h) + dot(t_up, above)).astype(jnp.bfloat16)
        pre = dot(e, w1e) + jnp.concatenate([h_src] * 3, axis=0) + dot(nxt, w1d)
        hid = jnp.maximum(pre, 0.0).astype(jnp.bfloat16)
        fresh = e.astype(jnp.float32) + layer_norm(dot(hid, w2))
        fresh = jnp.where(omask > 0.5, fresh, 0.0).astype(jnp.bfloat16)
        bottom = dot(bots, h).astype(jnp.bfloat16)
        pre_g = dot(g, w1e) + dot(below, w1s) + dot(bottom, w1d)
        hid_g = jnp.maximum(pre_g, 0.0).astype(jnp.bfloat16)
        ghost = g.astype(jnp.float32) + layer_norm(dot(hid_g, w2))
        ghost = jnp.where(lower > 0, ghost, 0.0).astype(jnp.bfloat16)
        total = dot(total_m, fresh) + dot(t_down, ghost)
        for d in range(3):
            e_out[d, b] = fresh[d * rows:(d + 1) * rows]
            g_out[d][b] = ghost[offsets[d]:offsets[d] + counts[d]]
        pre = dot(h, n1[:width]) + dot(total.astype(jnp.bfloat16), n1[width:]) + temb_ref[...]
        hid = jnp.maximum(pre, 0.0).astype(jnp.bfloat16)
        h_new = (h.astype(jnp.float32) + layer_norm(dot(hid, n2))).astype(jnp.bfloat16)
        h_out[b] = h_new
        bot_new = dot(bots, h_new).astype(jnp.bfloat16)
        top_new = dot(tops, h_new).astype(jnp.bfloat16)
        for d in range(3):
            bot_out[d][b] = bot_new[offsets[d]:offsets[d] + counts[d]]
            top_out[d][b] = top_new[offsets[d]:offsets[d] + counts[d]]


def whole(shape):
    return pl.BlockSpec(shape, lambda i, idx: (0,) * len(shape))


def run_layer(idx, h, e, ghosts, aboves, belows, temb, mine_all, other_all, scales, omask, mats):
    batch, rows, width = h.shape
    counts = [g.shape[1] for g in ghosts]
    out_shape = (
        [jax.ShapeDtypeStruct(h.shape, h.dtype), jax.ShapeDtypeStruct(e.shape, e.dtype)]
        + [jax.ShapeDtypeStruct(g.shape, g.dtype) for g in ghosts]
        + [jax.ShapeDtypeStruct((batch, c, width), h.dtype) for c in counts] * 2
    )
    flat_mats = list(mats)
    layer_block = (1,) + mine_all.shape[1:]
    operands = [h, e, *ghosts, *aboves, *belows, temb]
    in_specs = [whole(x.shape) for x in operands]
    in_specs += [pl.BlockSpec(layer_block, lambda i, idx: (idx[0], 0, 0))] * 2
    tail = [scales, omask, *flat_mats]
    in_specs += [whole(x.shape) for x in tail]
    grid_spec = pltpu.PrefetchScalarGridSpec(
        num_scalar_prefetch=1,
        grid=(1,),
        in_specs=in_specs,
        out_specs=[whole(o.shape) for o in out_shape],
    )
    res = pl.pallas_call(
        layer_kernel,
        out_shape=out_shape,
        grid_spec=grid_spec,
        input_output_aliases={1: 0, 2: 1, 3: 2, 4: 3, 5: 4},
    )(idx, *operands, mine_all, other_all, *tail)
    return res[0], res[1], tuple(res[2:5]), tuple(res[5:8]), tuple(res[8:11])


def local(
    nodes_in,
    edges_in,
    codes,
    type_table,
    order,
    edge_w1,
    edge_w2,
    node_w1,
    node_w2,
    edge_v1,
    edge_v2,
    node_v1,
    node_v2,
):
    section_count = lax.axis_size("section")
    section_id = lax.axis_index("section")
    count_z = lax.axis_size("space") // 16
    space_id = lax.axis_index("space")
    coords = (space_id // (4 * count_z), space_id // count_z % 4, space_id % count_z)
    counts = (4, 4, count_z)
    strides = (4 * count_z, count_z, 1)
    width = nodes_in.shape[-1]
    local_count = nodes_in.shape[0]
    rows = nodes_in.shape[1]
    batches = local_count * section_count
    type_ids = lax.broadcasted_iota(jnp.int32, (codes.shape[0], type_table.shape[0]), 1)
    one_hot = (codes[:, None] == type_ids).astype(jnp.float32)
    type_embed = jnp.sum(one_hot[:, :, None] * type_table[None, :, :], axis=1)
    divisor = jnp.float32(batches + 2 * section_count)

    mine = section_id * local_count + jnp.arange(local_count, dtype=jnp.int32)
    slots = jnp.arange(batches, dtype=jnp.int32)
    position = jnp.sum(
        jnp.where(order[None, :] == mine[:, None], slots[None, :], 0), axis=1
    )

    core = space_id % 2
    sizes = [w.shape[1] for w in (edge_w1, edge_w2, node_w1, node_w2)]
    halves = (
        jnp.concatenate([edge_w1[0], edge_w2[0], node_w1[0], node_w2[0]], axis=0),
        jnp.concatenate([edge_v1[0], edge_v2[0], node_v1[0], node_v2[0]], axis=0),
    )
    own_half = jnp.where(core == 0, halves[0], halves[1])
    space_count = lax.axis_size("space")
    ring = 4
    ring_stride = space_count // ring
    ring_pos = space_id // ring_stride
    pair_bit = space_id // 2 % 2
    group = 2 * ring
    chunk = own_half.shape[0] // group
    part_of = lambda ring_at, bit: ring_at * 2 + bit
    my_part = lax.dynamic_slice_in_dim(
        own_half, part_of(ring_pos, pair_bit) * chunk, chunk, axis=0
    )
    layers = jnp.zeros((section_count,) + my_part.shape, my_part.dtype)
    layers = lax.dynamic_update_slice_in_dim(layers, my_part[None], section_id, axis=0)
    for k in range(1, section_count):
        shift = [(i, (i + k) % section_count) for i in range(section_count)]
        layers = lax.dynamic_update_slice_in_dim(
            layers,
            lax.ppermute(my_part, "section", shift)[None],
            (section_id - k) % section_count,
            axis=0,
        )
    shape = (BX, BY, BZ)
    mats = plane_mats(shape)
    h0 = nodes_in
    e0 = jnp.transpose(edges_in, (1, 0, 2, 3))
    plane_counts = [rows // shape[a] for a in range(3)]
    plane_offsets = [sum(plane_counts[:a]) for a in range(3)]

    def split_planes(stacked):
        return tuple(
            stacked[:, plane_offsets[a]:plane_offsets[a] + plane_counts[a]] for a in range(3)
        )

    bot0 = split_planes(jnp.einsum("pr,brw->bpw", mats[2], h0).astype(jnp.bfloat16))
    top0 = split_planes(jnp.einsum("pr,brw->bpw", mats[3], h0).astype(jnp.bfloat16))
    ghosts0 = tuple(
        along_line(
            split_planes(jnp.einsum("pr,brw->bpw", mats[3], e0[a]).astype(jnp.bfloat16))[a],
            strides[a],
            strides[a],
            counts[a],
        )
        for a in range(3)
    )

    layers, ghosts0 = lax.optimization_barrier((layers, ghosts0))
    own_all = jnp.zeros((section_count, group * chunk, own_half.shape[1]), own_half.dtype)
    for dx in range(ring):
        for dz in range(2):
            if dx == 0 and dz == 0:
                got = layers
            else:
                moves = [
                    (i, (i // ring_stride + dx) % ring * ring_stride + ((i % ring_stride) ^ (2 * dz)))
                    for i in range(space_count)
                ]
                got = lax.ppermute(layers, "space", moves)
            source = part_of((ring_pos - dx) % ring, pair_bit ^ dz)
            own_all = lax.dynamic_update_slice_in_dim(own_all, got, source * chunk, axis=1)
    swap = [(i, i ^ 1) for i in range(space_count)]
    other_all = lax.ppermute(own_all, "space", swap)
    starts = [sum(sizes[:i]) for i in range(4)]

    grid_pos = np.stack(np.unravel_index(np.arange(rows), shape), axis=1)
    omask = jnp.stack(
        [
            jnp.broadcast_to(
                (coords[a] * shape[a] + grid_pos[:, a] < shape[a] * counts[a] - 1)[:, None],
                (rows, width),
            ).astype(jnp.float32)
            for a in range(3)
        ]
    ).reshape(3 * rows, width)
    lower_flags = [(coords[a] > 0).astype(jnp.int32) for a in range(3)]

    def layer_step(layer_id, carry):
        h, e, ghosts, bots, tops = carry
        scales = (position + 2 * section_count - 2 - layer_id).astype(jnp.float32) / divisor
        scales = jnp.broadcast_to(scales[:, None], (local_count, width))
        idx = jnp.stack([layer_id, core] + lower_flags).astype(jnp.int32)
        aboves = tuple(along_line(bots[a], -strides[a], strides[a], counts[a]) for a in range(3))
        belows = tuple(along_line(tops[a], strides[a], strides[a], counts[a]) for a in range(3))
        return run_layer(
            idx, h, e, ghosts, aboves, belows, type_embed, own_all, other_all, scales, omask, mats
        )

    h, _, _, _, _ = lax.fori_loop(
        0, section_count, layer_step, (h0, e0, ghosts0, bot0, top0)
    )
    return h


def solution(mesh):
    return jax.shard_map(
        local,
        mesh=mesh,
        in_specs=(
            P("section", "space", None),
            P("section", None, "space", None),
            P("space"),
            P(),
            P(),
            P("section", None, None),
            P("section", None, None),
            P("section", None, None),
            P("section", None, None),
            P("section", None, None),
            P("section", None, None),
            P("section", None, None),
            P("section", None, None),
        ),
        out_specs=P("section", "space", None),
        check_vma=False,
    )
```
